512 devices in a mesh: row: 32 (over x_lo, z), col: 16 (over x_hi, y, core).
Axes of the slice: x: 4 (x_hi: 2, x_lo: 2; x = x_hi * 2 + x_lo), y: 4, z: 16, core: 2. Of those that a mesh axis runs over, the one named last changes fastest.
Arguments:
- anc_inv: float32 [12288, 12288], P('row', 'col'), may hold values from -0.0546875 to 0.0546875
- factors_first: float32 [3, 256, 12288], P(None, 'row', 'col'), may hold values from -6 to 6
- factors_second: float32 [2, 256, 12288], P(None, 'row', 'col'), may hold values from -6 to 6
- lists_first: int32 [3, 36], replicated, may hold values from 0 to 47, as said below
- lists_second: int32 [2, 36], replicated, may hold values from 0 to 47, as said below
- parents: int32 [2], replicated, may hold values from 0 to 2, as said below
- parent_link: float32 [2, 256, 256], replicated, may hold values from -0.375 to 0.375
Outputs:
- first_cols: float32 [3, 256, 12288], P(None, 'col', 'row')
- second_cols: float32 [2, 256, 12288], P(None, 'col', 'row')
The draws below stay inside these ranges and needn't reach their ends.
Inputs may be any that keep to these rules, and one draw needn't show every extreme that they name: `lists_first`: each row holds 36 different tile indices. `lists_second`: each row holds 36 different tile indices. `parents`: the 2 entries are different first-generation indices.
All inputs are finite; a program needn't handle non-finite values.
Results may differ from the reference program's by a relative error of at most 0.000084.
Values sent between devices are 32-bit elements; how exact they have to be, the bound alone decides.
No kernel may reach another device: no remote copies, remote signals or barrier semaphores. Data moves between devices by JAX's collectives and lax.ppermute only.
A program may use at most 64 MiB of HBM per device.

```python
import jax
import jax.numpy as jnp
from jax import lax

ANC = 12288
W = 256
SA = 3
SN = 2
TILES = 48
R = 36


def pick_tiles(key, offset, count):
    member_keys = jax.random.split(jax.random.fold_in(key, offset), count)

    def single(member_key):
        return jax.random.permutation(member_key, TILES)[:R]
    return jax.vmap(single)(member_keys).astype(jnp.int32)


def draw_lists_first(key, part):
    return pick_tiles(key, 11, SA)


def draw_lists_second(key, part):
    return pick_tiles(key, 23, SN)


def draw_parents(key, part):
    return jax.random.permutation(jax.random.fold_in(key, 37), SA)[:SN].astype(jnp.int32)


def block_levels(stream_key, shape, pieces, smallest, largest):
    gain = 1.0
    for position, shards_of in pieces:
        steps = jax.random.uniform(jax.random.fold_in(jax.random.fold_in(stream_key, 6), position), (shards_of,), jnp.float32, smallest / len(pieces), largest / len(pieces))
        gain = gain * jnp.repeat(jnp.exp(steps), shape[position] // shards_of).reshape((-1,) + (1,) * (len(shape) - 1 - position))
    return gain


def scatter_about(own_key, shape, spread, limit, pieces=(), kind=jnp.bfloat16):
    values = spread * jax.random.normal(own_key, shape, jnp.float32)
    if pieces:
        values = values * block_levels(own_key, shape, pieces, -0.22, 0.18)
    return jnp.clip(values, -limit, limit).astype(kind)


def setup_inputs(seed: int = 0) -> dict:
    splits = jax.random.split(jax.random.key(seed), 8)
    return {
        "anc_inv": scatter_about(splits[0], (ANC, ANC), ANC ** -0.5, 0.0546875, ((0, 32), (1, 16)), jnp.float32),
        "factors_first": scatter_about(splits[1], (SA, W, ANC), 1.0, 6.0, ((1, 32), (2, 16)), jnp.float32),
        "factors_second": scatter_about(splits[2], (SN, W, ANC), 1.0, 6.0, ((1, 32), (2, 16)), jnp.float32),
        "lists_first": draw_lists_first(jax.random.fold_in(splits[7], 71), 0),
        "lists_second": draw_lists_second(jax.random.fold_in(splits[7], 71), 0),
        "parents": draw_parents(jax.random.fold_in(splits[7], 71), 0),
        "parent_link": scatter_about(splits[6], (SN, W, W), W ** -0.5, 0.375, (), jnp.float32),
    }


def tile_flags(block_lists, extent):
    tile_ids = jnp.arange(extent, dtype=jnp.int32) // W
    matches = block_lists[:, :, None] == tile_ids[None, None, :]
    return jnp.any(matches, axis=1).astype(jnp.float32)


def apply_inverse(anc_inv, panels):
    def single(panel):
        return lax.dot_general(panel, anc_inv, (((1,), (1,)), ((), ())), precision=lax.Precision.HIGHEST, preferred_element_type=jnp.float32)
    return lax.map(single, panels)


def reference(anc_inv, factors_first, factors_second, lists_first, lists_second, parents, parent_link):
    mask_first = tile_flags(lists_first, ANC)
    mask_second = tile_flags(lists_second, ANC)
    first_cols = -mask_first[:, None, :] * apply_inverse(anc_inv, factors_first * mask_first[:, None, :])
    chosen = jnp.take(first_cols, parents.astype(jnp.int32), axis=0)
    coupling = jnp.einsum("cqk,cqi->cki", parent_link, chosen, precision=lax.Precision.HIGHEST)
    second_sums = apply_inverse(anc_inv, factors_second * mask_second[:, None, :]) + coupling
    second_cols = -mask_second[:, None, :] * second_sums
    return (first_cols, second_cols)
```

```python
import jax
import jax.numpy as jnp
from jax import lax
from jax.sharding import PartitionSpec as P

highest = lax.Precision.HIGHEST


def tile_flags(block_lists, anchor, extent, tile_height):
    tile_ids = (anchor + jnp.arange(extent, dtype=jnp.int32)) // tile_height
    matches = block_lists[:, :, None] == tile_ids[None, None, :]
    return jnp.any(matches, axis=1).astype(jnp.float32)


def local(anc_inv, factors_first, factors_second, lists_first, lists_second, parents, parent_link):
    local_rows, local_cols = anc_inv.shape
    n_first = factors_first.shape[0]
    n_second = factors_second.shape[0]
    members = n_first + n_second
    share_rows = factors_first.shape[1]
    panel_width = parent_link.shape[1]
    row_anchor = lax.axis_index("row") * local_rows
    col_anchor = lax.axis_index("col") * local_cols
    out_first = tile_flags(lists_first, row_anchor, local_rows, panel_width)
    out_second = tile_flags(lists_second, row_anchor, local_rows, panel_width)
    panels = jnp.concatenate(
        [
            factors_first * tile_flags(lists_first, col_anchor, local_cols, panel_width)[:, None, :],
            factors_second * tile_flags(lists_second, col_anchor, local_cols, panel_width)[:, None, :],
        ],
        axis=0,
    )
    stacked = jnp.transpose(panels, (1, 0, 2)).reshape(share_rows, members * local_cols)
    gathered = lax.all_gather(stacked, "row", axis=0, tiled=True)
    gathered = gathered.reshape(panel_width, members, local_cols)
    partial_value = jnp.einsum(
        "kmj,ij->mki", gathered, anc_inv, precision=highest, preferred_element_type=jnp.float32
    )
    first_partial = partial_value[:n_first]
    second_partial = partial_value[n_first:]
    chosen = jnp.take(first_partial, parents, axis=0)
    chosen_mask = jnp.take(out_first, parents, axis=0)
    coupling = jnp.einsum("cqk,cqi->cki", parent_link, chosen, precision=highest)
    second_partial = second_partial - chosen_mask[:, None, :] * coupling
    combined = jnp.concatenate([first_partial, second_partial], axis=0)
    reduced = lax.psum_scatter(combined, "col", scatter_dimension=1, tiled=True)
    first_cols = -out_first[:, None, :] * reduced[:n_first]
    second_cols = -out_second[:, None, :] * reduced[n_first:]
    return (first_cols, second_cols)


def solution(mesh):
    in_specs = (P("row", "col"), P(None, "row", "col"), P(None, "row", "col"), P(), P(), P(), P())
    out_specs = (P(None, "col", "row"), P(None, "col", "row"))
    return jax.shard_map(local, mesh=mesh, in_specs=in_specs, out_specs=out_specs, check_vma=False)
```

```python
import jax
import jax.numpy as jnp
from jax import lax
from jax.sharding import PartitionSpec as P

highest = lax.Precision.HIGHEST

X_LO = 2
X_HI = 2
CORES = 2


def tile_flags(block_lists, anchor, extent, tile_height):
    tile_ids = (anchor + jnp.arange(extent, dtype=jnp.int32)) // tile_height
    matches = block_lists[:, :, None] == tile_ids[None, None, :]
    return jnp.any(matches, axis=1).astype(jnp.float32)


def shift_pairs(size, inner, stride, shift):
    pairs = []
    for p in range(size):
        q = (p // stride) % inner
        target = p + (((q + shift) % inner) - q) * stride
        pairs.append((p, target))
    return pairs


def gather_rows(block, n_row):
    nz = n_row // X_LO
    r = lax.axis_index("row")
    x_lo = r // nz
    z = r % nz
    partner = lax.ppermute(block, "row", [(p, (p + nz) % n_row) for p in range(n_row)])
    pair = jnp.where(x_lo == 0, jnp.stack([block, partner]), jnp.stack([partner, block]))
    up = shift_pairs(n_row, nz, 1, 1)
    down = shift_pairs(n_row, nz, 1, -1)
    pieces = [None] * nz
    pieces[0] = pair
    fwd = pair
    bwd = pair
    for t in range(1, nz // 2):
        fwd = lax.ppermute(fwd, "row", up)
        bwd = lax.ppermute(bwd, "row", down)
        pieces[nz - t] = fwd
        pieces[t] = bwd
    half = pair.shape[-1] // 2
    last_fwd = lax.ppermute(fwd[..., :half], "row", up)
    last_bwd = lax.ppermute(bwd[..., half:], "row", down)
    pieces[nz // 2] = jnp.concatenate([last_fwd, last_bwd], axis=-1)
    return jnp.stack(pieces), z


def reduce_cols(value, n_col):
    ny = n_col // (X_HI * CORES)
    c = lax.axis_index("col")
    core = c % CORES
    y = (c // CORES) % ny
    x_hi = c // (CORES * ny)
    send = jnp.take(value, 1 - core, axis=2)
    keep = jnp.take(value, core, axis=2)
    value = keep + lax.ppermute(send, "col", [(p, p ^ 1) for p in range(n_col)])
    rows = value.shape[2]
    upper = value[:, :, : rows // 2]
    lower = value[:, :, rows // 2 :]
    up = shift_pairs(n_col, ny, CORES, 1)
    down = shift_pairs(n_col, ny, CORES, -1)
    acc_up = jnp.take(upper, (y - 1) % ny, axis=1)
    acc_down = jnp.take(lower, (y + 1) % ny, axis=1)
    for s in range(1, ny):
        acc_up = lax.ppermute(acc_up, "col", up) + jnp.take(upper, (y - s - 1) % ny, axis=1)
        acc_down = lax.ppermute(acc_down, "col", down) + jnp.take(lower, (y + s + 1) % ny, axis=1)
    value = jnp.concatenate([acc_up, acc_down], axis=1)
    send = jnp.take(value, 1 - x_hi, axis=0)
    keep = jnp.take(value, x_hi, axis=0)
    half = n_col // X_HI
    return keep + lax.ppermute(send, "col", [(p, (p + half) % n_col) for p in range(n_col)])


def local(anc_inv, factors_first, factors_second, lists_first, lists_second, parents, parent_link):
    n_row = lax.axis_size("row")
    n_col = lax.axis_size("col")
    local_rows, local_cols = anc_inv.shape
    n_first = factors_first.shape[0]
    n_second = factors_second.shape[0]
    members = n_first + n_second
    share_rows = factors_first.shape[1]
    panel_width = parent_link.shape[1]
    nz = n_row // X_LO
    row_anchor = lax.axis_index("row") * local_rows
    col_anchor = lax.axis_index("col") * local_cols
    out_first = tile_flags(lists_first, row_anchor, local_rows, panel_width)
    out_second = tile_flags(lists_second, row_anchor, local_rows, panel_width)
    panels = jnp.concatenate(
        [
            factors_first * tile_flags(lists_first, col_anchor, local_cols, panel_width)[:, None, :],
            factors_second * tile_flags(lists_second, col_anchor, local_cols, panel_width)[:, None, :],
        ],
        axis=0,
    )
    stacked = jnp.transpose(panels, (1, 0, 2)).reshape(share_rows, members * local_cols)
    pieces, z = gather_rows(stacked, n_row)
    pieces = pieces.reshape(nz, X_LO, share_rows, members, local_cols)
    partial_value = jnp.einsum(
        "tlkmj,ij->ltkmi", pieces, anc_inv, precision=highest, preferred_element_type=jnp.float32
    )
    partial_value = jnp.roll(partial_value, z, axis=1)
    partial_value = partial_value.reshape(panel_width, members, local_rows)
    first_partial = partial_value[:, :n_first]
    chosen = jnp.take(first_partial, parents, axis=1)
    chosen_mask = jnp.take(out_first, parents, axis=0)
    coupling = jnp.einsum("cqk,qci->kci", parent_link, chosen, precision=highest)
    second_partial = partial_value[:, n_first:] - chosen_mask[None, :, :] * coupling
    combined = jnp.concatenate([first_partial, second_partial], axis=1)
    ny = n_col // (X_HI * CORES)
    combined = combined.reshape(X_HI, ny, CORES, panel_width // n_col, members, local_rows)
    reduced = reduce_cols(combined, n_col)
    reduced = jnp.transpose(reduced, (1, 0, 2))
    first_cols = -out_first[:, None, :] * reduced[:n_first]
    second_cols = -out_second[:, None, :] * reduced[n_first:]
    return (first_cols, second_cols)


def solution(mesh):
    in_specs = (P("row", "col"), P(None, "row", "col"), P(None, "row", "col"), P(), P(), P(), P())
    out_specs = (P(None, "col", "row"), P(None, "col", "row"))
    return jax.shard_map(local, mesh=mesh, in_specs=in_specs, out_specs=out_specs, check_vma=False)
```

```python
import jax
import jax.numpy as jnp
from jax import lax
from jax.sharding import PartitionSpec as P

highest = lax.Precision.HIGHEST

X_LO = 2
X_HI = 2
CORES = 2


def tile_flags(block_lists, anchor, extent, tile_height):
    tile_ids = (anchor + jnp.arange(extent, dtype=jnp.int32)) // tile_height
    matches = block_lists[:, :, None] == tile_ids[None, None, :]
    return jnp.any(matches, axis=1).astype(jnp.float32)


def shift_pairs(size, inner, stride, shift):
    pairs = []
    for p in range(size):
        q = (p // stride) % inner
        target = p + (((q + shift) % inner) - q) * stride
        pairs.append((p, target))
    return pairs


def gather_rows(block, n_row):
    nz = n_row // X_LO
    r = lax.axis_index("row")
    x_lo = r // nz
    z = r % nz
    partner = lax.ppermute(block, "row", [(p, (p + nz) % n_row) for p in range(n_row)])
    pair = jnp.where(x_lo == 0, jnp.stack([block, partner]), jnp.stack([partner, block]))
    up = shift_pairs(n_row, nz, 1, 1)
    down = shift_pairs(n_row, nz, 1, -1)
    pieces = [None] * nz
    pieces[0] = pair
    fwd = pair
    bwd = pair
    for t in range(1, nz // 2):
        fwd = lax.ppermute(fwd, "row", up)
        bwd = lax.ppermute(bwd, "row", down)
        pieces[nz - t] = fwd
        pieces[t] = bwd
    half = pair.shape[-1] // 2
    last_fwd = lax.ppermute(fwd[..., :half], "row", up)
    last_bwd = lax.ppermute(bwd[..., half:], "row", down)
    pieces[nz // 2] = jnp.concatenate([last_fwd, last_bwd], axis=-1)
    return jnp.stack(pieces), z


def reduce_cols(value, n_col):
    ny = n_col // (X_HI * CORES)
    c = lax.axis_index("col")
    core = c % CORES
    y = (c // CORES) % ny
    x_hi = c // (CORES * ny)
    send = jnp.take(value, 1 - core, axis=2)
    keep = jnp.take(value, core, axis=2)
    value = keep + lax.ppermute(send, "col", [(p, p ^ 1) for p in range(n_col)])
    rows = value.shape[2]
    upper = value[:, :, : rows // 2]
    lower = value[:, :, rows // 2 :]
    up = shift_pairs(n_col, ny, CORES, 1)
    down = shift_pairs(n_col, ny, CORES, -1)
    acc_up = jnp.take(upper, (y - 1) % ny, axis=1)
    acc_down = jnp.take(lower, (y + 1) % ny, axis=1)
    for s in range(1, ny):
        acc_up = lax.ppermute(acc_up, "col", up) + jnp.take(upper, (y - s - 1) % ny, axis=1)
        acc_down = lax.ppermute(acc_down, "col", down) + jnp.take(lower, (y + s + 1) % ny, axis=1)
    value = jnp.concatenate([acc_up, acc_down], axis=1)
    send = jnp.take(value, 1 - x_hi, axis=0)
    keep = jnp.take(value, x_hi, axis=0)
    half = n_col // X_HI
    return keep + lax.ppermute(send, "col", [(p, (p + half) % n_col) for p in range(n_col)])


def local(anc_inv, factors_first, factors_second, lists_first, lists_second, parents, parent_link):
    n_row = lax.axis_size("row")
    n_col = lax.axis_size("col")
    local_rows, local_cols = anc_inv.shape
    n_first = factors_first.shape[0]
    n_second = factors_second.shape[0]
    members = n_first + n_second
    share_rows = factors_first.shape[1]
    panel_width = parent_link.shape[1]
    nz = n_row // X_LO
    row_anchor = lax.axis_index("row") * local_rows
    col_anchor = lax.axis_index("col") * local_cols
    out_first = tile_flags(lists_first, row_anchor, local_rows, panel_width)
    out_second = tile_flags(lists_second, row_anchor, local_rows, panel_width)
    panels = jnp.concatenate([factors_first, factors_second], axis=0)
    stacked = jnp.transpose(panels, (1, 0, 2)).reshape(share_rows, members * local_cols)
    pieces, z = gather_rows(stacked, n_row)
    col_mask = jnp.concatenate(
        [
            tile_flags(lists_first, col_anchor, local_cols, panel_width),
            tile_flags(lists_second, col_anchor, local_cols, panel_width),
        ],
        axis=0,
    )
    pieces = pieces.reshape(nz, X_LO, share_rows, members, local_cols) * col_mask
    partial_value = jnp.einsum(
        "tlkmj,ij->ltkmi", pieces, anc_inv, precision=highest, preferred_element_type=jnp.float32
    )
    partial_value = jnp.roll(partial_value, z, axis=1)
    partial_value = partial_value.reshape(panel_width, members, local_rows)
    first_partial = partial_value[:, :n_first]
    chosen = jnp.take(first_partial, parents, axis=1)
    chosen_mask = jnp.take(out_first, parents, axis=0)
    coupling = jnp.einsum("cqk,qci->kci", parent_link, chosen, precision=highest)
    second_partial = partial_value[:, n_first:] - chosen_mask[None, :, :] * coupling
    combined = jnp.concatenate([first_partial, second_partial], axis=1)
    combined = combined.reshape(n_col, panel_width // n_col, members, local_rows)
    reduced = jnp.sum(lax.all_to_all(combined, "col", 0, 0, tiled=True), axis=0)
    reduced = jnp.transpose(reduced, (1, 0, 2))
    first_cols = -out_first[:, None, :] * reduced[:n_first]
    second_cols = -out_second[:, None, :] * reduced[n_first:]
    return (first_cols, second_cols)


def solution(mesh):
    in_specs = (P("row", "col"), P(None, "row", "col"), P(None, "row", "col"), P(), P(), P(), P())
    out_specs = (P(None, "col", "row"), P(None, "col", "row"))
    return jax.shard_map(local, mesh=mesh, in_specs=in_specs, out_specs=out_specs, check_vma=False)
```

```python
import jax
import jax.numpy as jnp
from jax import lax
from jax.sharding import PartitionSpec as P

highest = lax.Precision.HIGHEST

X_LO = 2
X_HI = 2
CORES = 2


def tile_flags(block_lists, anchor, extent, tile_height):
    tile_ids = (anchor + jnp.arange(extent, dtype=jnp.int32)) // tile_height
    matches = block_lists[:, :, None] == tile_ids[None, None, :]
    return jnp.any(matches, axis=1).astype(jnp.float32)


def shift_pairs(size, inner, stride, shift):
    pairs = []
    for p in range(size):
        q = (p // stride) % inner
        target = p + (((q + shift) % inner) - q) * stride
        pairs.append((p, target))
    return pairs


def gather_rows(block, n_row):
    nz = n_row // X_LO
    r = lax.axis_index("row")
    x_lo = r // nz
    z = r % nz
    partner = lax.ppermute(block, "row", [(p, (p + nz) % n_row) for p in range(n_row)])
    pair = jnp.where(x_lo == 0, jnp.stack([block, partner]), jnp.stack([partner, block]))
    up = shift_pairs(n_row, nz, 1, 1)
    down = shift_pairs(n_row, nz, 1, -1)
    pieces = [None] * nz
    pieces[0] = pair
    fwd = pair
    bwd = pair
    for t in range(1, nz // 2):
        fwd = lax.ppermute(fwd, "row", up)
        bwd = lax.ppermute(bwd, "row", down)
        pieces[nz - t] = fwd
        pieces[t] = bwd
    half = pair.shape[-1] // 2
    last_fwd = lax.ppermute(fwd[..., :half], "row", up)
    last_bwd = lax.ppermute(bwd[..., half:], "row", down)
    pieces[nz // 2] = jnp.concatenate([last_fwd, last_bwd], axis=-1)
    return jnp.stack(pieces), z


def reduce_cols(value, n_col):
    ny = n_col // (X_HI * CORES)
    c = lax.axis_index("col")
    core = c % CORES
    y = (c // CORES) % ny
    x_hi = c // (CORES * ny)
    send = jnp.take(value, 1 - core, axis=2)
    keep = jnp.take(value, core, axis=2)
    value = keep + lax.ppermute(send, "col", [(p, p ^ 1) for p in range(n_col)])
    total = value[x_hi, y]
    for dx in range(X_HI):
        for dy in range(ny):
            if dx == 0 and dy == 0:
                continue
            pairs = []
            for p in range(n_col):
                px, py, pc = p // (CORES * ny), (p // CORES) % ny, p % CORES
                pairs.append((p, ((px + dx) % X_HI * ny + (py + dy) % ny) * CORES + pc))
            block = value[(x_hi + dx) % X_HI, (y + dy) % ny]
            total = total + lax.ppermute(block, "col", pairs)
    return total


def local(anc_inv, factors_first, factors_second, lists_first, lists_second, parents, parent_link):
    n_row = lax.axis_size("row")
    n_col = lax.axis_size("col")
    local_rows, local_cols = anc_inv.shape
    n_first = factors_first.shape[0]
    n_second = factors_second.shape[0]
    members = n_first + n_second
    share_rows = factors_first.shape[1]
    panel_width = parent_link.shape[1]
    nz = n_row // X_LO
    row_anchor = lax.axis_index("row") * local_rows
    col_anchor = lax.axis_index("col") * local_cols
    out_first = tile_flags(lists_first, row_anchor, local_rows, panel_width)
    out_second = tile_flags(lists_second, row_anchor, local_rows, panel_width)
    panels = jnp.concatenate([factors_first, factors_second], axis=0)
    stacked = jnp.transpose(panels, (1, 0, 2)).reshape(share_rows, members * local_cols)
    pieces, z = gather_rows(stacked, n_row)
    col_mask = jnp.concatenate(
        [
            tile_flags(lists_first, col_anchor, local_cols, panel_width),
            tile_flags(lists_second, col_anchor, local_cols, panel_width),
        ],
        axis=0,
    )
    pieces = pieces.reshape(nz, X_LO, share_rows, members, local_cols) * col_mask
    partial_value = jnp.einsum(
        "tlkmj,ij->ltkmi", pieces, anc_inv, precision=highest, preferred_element_type=jnp.float32
    )
    partial_value = jnp.roll(partial_value, z, axis=1)
    partial_value = partial_value.reshape(panel_width, members, local_rows)
    first_partial = partial_value[:, :n_first]
    chosen = jnp.take(first_partial, parents, axis=1)
    chosen_mask = jnp.take(out_first, parents, axis=0)
    coupling = jnp.einsum("cqk,qci->kci", parent_link, chosen, precision=highest)
    second_partial = partial_value[:, n_first:] - chosen_mask[None, :, :] * coupling
    combined = jnp.concatenate([first_partial, second_partial], axis=1)
    ny = n_col // (X_HI * CORES)
    combined = combined.reshape(X_HI, ny, CORES, panel_width // n_col, members, local_rows)
    reduced = reduce_cols(combined, n_col)
    reduced = jnp.transpose(reduced, (1, 0, 2))
    first_cols = -out_first[:, None, :] * reduced[:n_first]
    second_cols = -out_second[:, None, :] * reduced[n_first:]
    return (first_cols, second_cols)


def solution(mesh):
    in_specs = (P("row", "col"), P(None, "row", "col"), P(None, "row", "col"), P(), P(), P(), P())
    out_specs = (P(None, "col", "row"), P(None, "col", "row"))
    return jax.shard_map(local, mesh=mesh, in_specs=in_specs, out_specs=out_specs, check_vma=False)
```

```python
import jax
import jax.numpy as jnp
from jax import lax
from jax.sharding import PartitionSpec as P

highest = lax.Precision.HIGHEST

X_LO = 2
X_HI = 2
CORES = 2
SC_MEMBERS = 2


def tile_flags(block_lists, anchor, extent, tile_height):
    tile_ids = (anchor + jnp.arange(extent, dtype=jnp.int32)) // tile_height
    matches = block_lists[:, :, None] == tile_ids[None, None, :]
    return jnp.any(matches, axis=1).astype(jnp.float32)


def shift_pairs(size, inner, stride, shift):
    pairs = []
    for p in range(size):
        q = (p // stride) % inner
        target = p + (((q + shift) % inner) - q) * stride
        pairs.append((p, target))
    return pairs


def gather_rows(block, n_row):
    nz = n_row // X_LO
    r = lax.axis_index("row")
    x_lo = r // nz
    z = r % nz
    partner = lax.ppermute(block, "row", [(p, (p + nz) % n_row) for p in range(n_row)])
    pair = jnp.where(x_lo == 0, jnp.stack([block, partner]), jnp.stack([partner, block]))
    up = shift_pairs(n_row, nz, 1, 1)
    down = shift_pairs(n_row, nz, 1, -1)
    pieces = [None] * nz
    pieces[0] = pair
    fwd = pair
    bwd = pair
    for t in range(1, nz // 2):
        fwd = lax.ppermute(fwd, "row", up)
        bwd = lax.ppermute(bwd, "row", down)
        pieces[nz - t] = fwd
        pieces[t] = bwd
    half = pair.shape[-1] // 2
    last_fwd = lax.ppermute(fwd[..., :half], "row", up)
    last_bwd = lax.ppermute(bwd[..., half:], "row", down)
    pieces[nz // 2] = jnp.concatenate([last_fwd, last_bwd], axis=-1)
    return jnp.stack(pieces), z


def reduce_cols(value, n_col):
    ny = n_col // (X_HI * CORES)
    c = lax.axis_index("col")
    core = c % CORES
    y = (c // CORES) % ny
    x_hi = c // (CORES * ny)
    send = jnp.take(value, 1 - core, axis=2)
    keep = jnp.take(value, core, axis=2)
    value = keep + lax.ppermute(send, "col", [(p, p ^ 1) for p in range(n_col)])
    rows = value.shape[2]
    upper = value[:, :, : rows // 2]
    lower = value[:, :, rows // 2 :]
    up = shift_pairs(n_col, ny, CORES, 1)
    down = shift_pairs(n_col, ny, CORES, -1)
    acc_up = jnp.take(upper, (y - 1) % ny, axis=1)
    acc_down = jnp.take(lower, (y + 1) % ny, axis=1)
    for s in range(1, ny):
        acc_up = lax.ppermute(acc_up, "col", up) + jnp.take(upper, (y - s - 1) % ny, axis=1)
        acc_down = lax.ppermute(acc_down, "col", down) + jnp.take(lower, (y + s + 1) % ny, axis=1)
    value = jnp.concatenate([acc_up, acc_down], axis=1)
    send = jnp.take(value, 1 - x_hi, axis=0)
    keep = jnp.take(value, x_hi, axis=0)
    half = n_col // X_HI
    return keep + lax.ppermute(send, "col", [(p, (p + half) % n_col) for p in range(n_col)])


def local(anc_inv, factors_first, factors_second, lists_first, lists_second, parents, parent_link):
    n_row = lax.axis_size("row")
    n_col = lax.axis_size("col")
    local_rows, local_cols = anc_inv.shape
    n_first = factors_first.shape[0]
    n_second = factors_second.shape[0]
    members = n_first + n_second
    share_rows = factors_first.shape[1]
    panel_width = parent_link.shape[1]
    nz = n_row // X_LO
    row_anchor = lax.axis_index("row") * local_rows
    col_anchor = lax.axis_index("col") * local_cols
    out_first = tile_flags(lists_first, row_anchor, local_rows, panel_width)
    out_second = tile_flags(lists_second, row_anchor, local_rows, panel_width)
    panels = jnp.concatenate([factors_first, factors_second], axis=0)
    native = jnp.transpose(panels[:SC_MEMBERS], (1, 0, 2)).reshape(share_rows, SC_MEMBERS * local_cols)
    native = lax.all_gather(native, "row", axis=0, tiled=True).reshape(panel_width, SC_MEMBERS, local_cols)
    ring_members = members - SC_MEMBERS
    stacked = jnp.transpose(panels[SC_MEMBERS:], (1, 0, 2)).reshape(share_rows, ring_members * local_cols)
    pieces, z = gather_rows(stacked, n_row)
    col_mask = jnp.concatenate(
        [
            tile_flags(lists_first, col_anchor, local_cols, panel_width),
            tile_flags(lists_second, col_anchor, local_cols, panel_width),
        ],
        axis=0,
    )
    native = native * col_mask[:SC_MEMBERS]
    pieces = pieces.reshape(nz, X_LO, share_rows, ring_members, local_cols) * col_mask[SC_MEMBERS:]
    native_value = jnp.einsum(
        "kmj,ij->kmi", native, anc_inv, precision=highest, preferred_element_type=jnp.float32
    )
    ring_value = jnp.einsum(
        "tlkmj,ij->ltkmi", pieces, anc_inv, precision=highest, preferred_element_type=jnp.float32
    )
    ring_value = jnp.roll(ring_value, z, axis=1).reshape(panel_width, ring_members, local_rows)
    partial_value = jnp.concatenate([native_value, ring_value], axis=1)
    first_partial = partial_value[:, :n_first]
    chosen = jnp.take(first_partial, parents, axis=1)
    chosen_mask = jnp.take(out_first, parents, axis=0)
    coupling = jnp.einsum("cqk,qci->kci", parent_link, chosen, precision=highest)
    second_partial = partial_value[:, n_first:] - chosen_mask[None, :, :] * coupling
    combined = jnp.concatenate([first_partial, second_partial], axis=1)
    combined = combined.reshape(n_col, panel_width // n_col, members, local_rows)
    reduced = jnp.sum(lax.all_to_all(combined, "col", 0, 0, tiled=True), axis=0)
    reduced = jnp.transpose(reduced, (1, 0, 2))
    first_cols = -out_first[:, None, :] * reduced[:n_first]
    second_cols = -out_second[:, None, :] * reduced[n_first:]
    return (first_cols, second_cols)


def solution(mesh):
    in_specs = (P("row", "col"), P(None, "row", "col"), P(None, "row", "col"), P(), P(), P(), P())
    out_specs = (P(None, "col", "row"), P(None, "col", "row"))
    return jax.shard_map(local, mesh=mesh, in_specs=in_specs, out_specs=out_specs, check_vma=False)
```

```python
import jax
import jax.numpy as jnp
from jax import lax
from jax.sharding import PartitionSpec as P

highest = lax.Precision.HIGHEST

X_LO = 2
X_HI = 2
CORES = 2


def tile_flags(block_lists, anchor, extent, tile_height):
    tile_ids = (anchor + jnp.arange(extent, dtype=jnp.int32)) // tile_height
    matches = block_lists[:, :, None] == tile_ids[None, None, :]
    return jnp.any(matches, axis=1).astype(jnp.float32)


def shift_pairs(size, inner, stride, shift):
    pairs = []
    for p in range(size):
        q = (p // stride) % inner
        target = p + (((q + shift) % inner) - q) * stride
        pairs.append((p, target))
    return pairs


def gather_rows(block, n_row):
    nz = n_row // X_LO
    r = lax.axis_index("row")
    x_lo = r // nz
    z = r % nz
    partner = lax.ppermute(block, "row", [(p, (p + nz) % n_row) for p in range(n_row)])
    pair = jnp.where(x_lo == 0, jnp.stack([block, partner]), jnp.stack([partner, block]))
    pieces = [None] * nz
    pieces[0] = pair
    steps = nz // 4
    half = pair.shape[-1] // 2
    lane_up = pair
    lane_down = pair
    for t in range(1, steps + 1):
        pieces[nz - (2 * t - 1)] = lax.ppermute(lane_up, "row", shift_pairs(n_row, nz, 1, 1))
        pieces[2 * t - 1] = lax.ppermute(lane_down, "row", shift_pairs(n_row, nz, 1, -1))
        if t < steps:
            lane_up = lax.ppermute(lane_up, "row", shift_pairs(n_row, nz, 1, 2))
            lane_down = lax.ppermute(lane_down, "row", shift_pairs(n_row, nz, 1, -2))
            pieces[nz - 2 * t] = lane_up
            pieces[2 * t] = lane_down
        else:
            last_up = lax.ppermute(lane_up[..., :half], "row", shift_pairs(n_row, nz, 1, 2))
            last_down = lax.ppermute(lane_down[..., half:], "row", shift_pairs(n_row, nz, 1, -2))
            pieces[nz // 2] = jnp.concatenate([last_up, last_down], axis=-1)
    return jnp.stack(pieces), z


def reduce_cols(value, n_col):
    ny = n_col // (X_HI * CORES)
    c = lax.axis_index("col")
    core = c % CORES
    y = (c // CORES) % ny
    x_hi = c // (CORES * ny)
    send = jnp.take(value, 1 - core, axis=2)
    keep = jnp.take(value, core, axis=2)
    value = keep + lax.ppermute(send, "col", [(p, p ^ 1) for p in range(n_col)])
    rows = value.shape[2]
    upper = value[:, :, : rows // 2]
    lower = value[:, :, rows // 2 :]
    up = shift_pairs(n_col, ny, CORES, 1)
    down = shift_pairs(n_col, ny, CORES, -1)
    acc_up = jnp.take(upper, (y - 1) % ny, axis=1)
    acc_down = jnp.take(lower, (y + 1) % ny, axis=1)
    for s in range(1, ny):
        acc_up = lax.ppermute(acc_up, "col", up) + jnp.take(upper, (y - s - 1) % ny, axis=1)
        acc_down = lax.ppermute(acc_down, "col", down) + jnp.take(lower, (y + s + 1) % ny, axis=1)
    value = jnp.concatenate([acc_up, acc_down], axis=1)
    send = jnp.take(value, 1 - x_hi, axis=0)
    keep = jnp.take(value, x_hi, axis=0)
    half = n_col // X_HI
    return keep + lax.ppermute(send, "col", [(p, (p + half) % n_col) for p in range(n_col)])


def local(anc_inv, factors_first, factors_second, lists_first, lists_second, parents, parent_link):
    n_row = lax.axis_size("row")
    n_col = lax.axis_size("col")
    local_rows, local_cols = anc_inv.shape
    n_first = factors_first.shape[0]
    n_second = factors_second.shape[0]
    members = n_first + n_second
    share_rows = factors_first.shape[1]
    panel_width = parent_link.shape[1]
    nz = n_row // X_LO
    row_anchor = lax.axis_index("row") * local_rows
    col_anchor = lax.axis_index("col") * local_cols
    out_first = tile_flags(lists_first, row_anchor, local_rows, panel_width)
    out_second = tile_flags(lists_second, row_anchor, local_rows, panel_width)
    panels = jnp.concatenate([factors_first, factors_second], axis=0)
    stacked = jnp.transpose(panels, (1, 0, 2)).reshape(share_rows, members * local_cols)
    pieces, z = gather_rows(stacked, n_row)
    col_mask = jnp.concatenate(
        [
            tile_flags(lists_first, col_anchor, local_cols, panel_width),
            tile_flags(lists_second, col_anchor, local_cols, panel_width),
        ],
        axis=0,
    )
    pieces = pieces.reshape(nz, X_LO, share_rows, members, local_cols) * col_mask
    partial_value = jnp.einsum(
        "tlkmj,ij->ltkmi", pieces, anc_inv, precision=highest, preferred_element_type=jnp.float32
    )
    partial_value = jnp.roll(partial_value, z, axis=1)
    partial_value = partial_value.reshape(panel_width, members, local_rows)
    first_partial = partial_value[:, :n_first]
    chosen = jnp.take(first_partial, parents, axis=1)
    chosen_mask = jnp.take(out_first, parents, axis=0)
    coupling = jnp.einsum("cqk,qci->kci", parent_link, chosen, precision=highest)
    second_partial = partial_value[:, n_first:] - chosen_mask[None, :, :] * coupling
    combined = jnp.concatenate([first_partial, second_partial], axis=1)
    combined = combined.reshape(n_col, panel_width // n_col, members, local_rows)
    reduced = jnp.sum(lax.all_to_all(combined, "col", 0, 0, tiled=True), axis=0)
    reduced = jnp.transpose(reduced, (1, 0, 2))
    first_cols = -out_first[:, None, :] * reduced[:n_first]
    second_cols = -out_second[:, None, :] * reduced[n_first:]
    return (first_cols, second_cols)


def solution(mesh):
    in_specs = (P("row", "col"), P(None, "row", "col"), P(None, "row", "col"), P(), P(), P(), P())
    out_specs = (P(None, "col", "row"), P(None, "col", "row"))
    return jax.shard_map(local, mesh=mesh, in_specs=in_specs, out_specs=out_specs, check_vma=False)
```

```python
import jax
import jax.numpy as jnp
from jax import lax
from jax.sharding import PartitionSpec as P

highest = lax.Precision.HIGHEST

X_LO = 2
X_HI = 2
CORES = 2


def tile_flags(block_lists, anchor, extent, tile_height):
    tile_ids = (anchor + jnp.arange(extent, dtype=jnp.int32)) // tile_height
    matches = block_lists[:, :, None] == tile_ids[None, None, :]
    return jnp.any(matches, axis=1).astype(jnp.float32)


def shift_pairs(size, inner, stride, shift):
    pairs = []
    for p in range(size):
        q = (p // stride) % inner
        target = p + (((q + shift) % inner) - q) * stride
        pairs.append((p, target))
    return pairs


def gather_rows(block, n_row):
    nz = n_row // X_LO
    r = lax.axis_index("row")
    x_lo = r // nz
    z = r % nz
    partner = lax.ppermute(block, "row", [(p, (p + nz) % n_row) for p in range(n_row)])
    pair = jnp.where(x_lo == 0, jnp.stack([block, partner]), jnp.stack([partner, block]))
    pieces = [None] * nz
    pieces[0] = pair
    steps = nz // 4
    half = pair.shape[-1] // 2
    lane_up = pair
    lane_down = pair
    for t in range(1, steps + 1):
        pieces[nz - (2 * t - 1)] = lax.ppermute(lane_up, "row", shift_pairs(n_row, nz, 1, 1))
        pieces[2 * t - 1] = lax.ppermute(lane_down, "row", shift_pairs(n_row, nz, 1, -1))
        if t < steps:
            lane_up = lax.ppermute(lane_up, "row", shift_pairs(n_row, nz, 1, 2))
            lane_down = lax.ppermute(lane_down, "row", shift_pairs(n_row, nz, 1, -2))
            pieces[nz - 2 * t] = lane_up
            pieces[2 * t] = lane_down
        else:
            last_up = lax.ppermute(lane_up[..., :half], "row", shift_pairs(n_row, nz, 1, 2))
            last_down = lax.ppermute(lane_down[..., half:], "row", shift_pairs(n_row, nz, 1, -2))
            pieces[nz // 2] = jnp.concatenate([last_up, last_down], axis=-1)
    return pieces, z


def reduce_cols(value, n_col):
    ny = n_col // (X_HI * CORES)
    c = lax.axis_index("col")
    core = c % CORES
    y = (c // CORES) % ny
    x_hi = c // (CORES * ny)
    send = jnp.take(value, 1 - core, axis=2)
    keep = jnp.take(value, core, axis=2)
    value = keep + lax.ppermute(send, "col", [(p, p ^ 1) for p in range(n_col)])
    rows = value.shape[2]
    upper = value[:, :, : rows // 2]
    lower = value[:, :, rows // 2 :]
    up = shift_pairs(n_col, ny, CORES, 1)
    down = shift_pairs(n_col, ny, CORES, -1)
    acc_up = jnp.take(upper, (y - 1) % ny, axis=1)
    acc_down = jnp.take(lower, (y + 1) % ny, axis=1)
    for s in range(1, ny):
        acc_up = lax.ppermute(acc_up, "col", up) + jnp.take(upper, (y - s - 1) % ny, axis=1)
        acc_down = lax.ppermute(acc_down, "col", down) + jnp.take(lower, (y + s + 1) % ny, axis=1)
    value = jnp.concatenate([acc_up, acc_down], axis=1)
    send = jnp.take(value, 1 - x_hi, axis=0)
    keep = jnp.take(value, x_hi, axis=0)
    half = n_col // X_HI
    return keep + lax.ppermute(send, "col", [(p, (p + half) % n_col) for p in range(n_col)])


def local(anc_inv, factors_first, factors_second, lists_first, lists_second, parents, parent_link):
    n_row = lax.axis_size("row")
    n_col = lax.axis_size("col")
    local_rows, local_cols = anc_inv.shape
    n_first = factors_first.shape[0]
    n_second = factors_second.shape[0]
    members = n_first + n_second
    share_rows = factors_first.shape[1]
    panel_width = parent_link.shape[1]
    nz = n_row // X_LO
    row_anchor = lax.axis_index("row") * local_rows
    col_anchor = lax.axis_index("col") * local_cols
    out_first = tile_flags(lists_first, row_anchor, local_rows, panel_width)
    out_second = tile_flags(lists_second, row_anchor, local_rows, panel_width)
    panels = jnp.concatenate([factors_first, factors_second], axis=0)
    stacked = jnp.transpose(panels, (1, 0, 2)).reshape(share_rows, members * local_cols)
    pieces, z = gather_rows(stacked, n_row)
    col_mask = jnp.concatenate(
        [
            tile_flags(lists_first, col_anchor, local_cols, panel_width),
            tile_flags(lists_second, col_anchor, local_cols, panel_width),
        ],
        axis=0,
    )

    def apply_piece(piece):
        piece = piece.reshape(X_LO, share_rows, members, local_cols) * col_mask
        return jnp.einsum(
            "lkmj,ij->lkmi", piece, anc_inv, precision=highest, preferred_element_type=jnp.float32
        )

    partial_value = jnp.stack([apply_piece(piece) for piece in pieces], axis=1)
    partial_value = jnp.roll(partial_value, z, axis=1)
    partial_value = partial_value.reshape(panel_width, members, local_rows)
    first_partial = partial_value[:, :n_first]
    chosen = jnp.take(first_partial, parents, axis=1)
    chosen_mask = jnp.take(out_first, parents, axis=0)
    coupling = jnp.einsum("cqk,qci->kci", parent_link, chosen, precision=highest)
    second_partial = partial_value[:, n_first:] - chosen_mask[None, :, :] * coupling
    combined = jnp.concatenate([first_partial, second_partial], axis=1)
    combined = combined.reshape(n_col, panel_width // n_col, members, local_rows)
    reduced = jnp.sum(lax.all_to_all(combined, "col", 0, 0, tiled=True), axis=0)
    reduced = jnp.transpose(reduced, (1, 0, 2))
    first_cols = -out_first[:, None, :] * reduced[:n_first]
    second_cols = -out_second[:, None, :] * reduced[n_first:]
    return (first_cols, second_cols)


def solution(mesh):
    in_specs = (P("row", "col"), P(None, "row", "col"), P(None, "row", "col"), P(), P(), P(), P())
    out_specs = (P(None, "col", "row"), P(None, "col", "row"))
    return jax.shard_map(local, mesh=mesh, in_specs=in_specs, out_specs=out_specs, check_vma=False)
```

```python
import jax
import jax.numpy as jnp
from jax import lax
from jax.sharding import PartitionSpec as P

highest = lax.Precision.HIGHEST

X_LO = 2
X_HI = 2
CORES = 2


def tile_flags(block_lists, anchor, extent, tile_height):
    tile_ids = (anchor + jnp.arange(extent, dtype=jnp.int32)) // tile_height
    matches = block_lists[:, :, None] == tile_ids[None, None, :]
    return jnp.any(matches, axis=1).astype(jnp.float32)


def shift_pairs(size, inner, stride, shift):
    pairs = []
    for p in range(size):
        q = (p // stride) % inner
        target = p + (((q + shift) % inner) - q) * stride
        pairs.append((p, target))
    return pairs


def gather_rows(block, n_row):
    nz = n_row // X_LO
    r = lax.axis_index("row")
    x_lo = r // nz
    z = r % nz
    partner = lax.ppermute(block, "row", [(p, (p + nz) % n_row) for p in range(n_row)])
    pair = jnp.where(x_lo == 0, jnp.stack([block, partner]), jnp.stack([partner, block]))
    pieces = [None] * nz
    pieces[0] = pair
    steps = nz // 4
    half = pair.shape[-1] // 2
    lane_up = pair
    lane_down = pair
    for t in range(1, steps + 1):
        pieces[nz - (2 * t - 1)] = lax.ppermute(lane_up, "row", shift_pairs(n_row, nz, 1, 1))
        pieces[2 * t - 1] = lax.ppermute(lane_down, "row", shift_pairs(n_row, nz, 1, -1))
        if t < steps:
            lane_up = lax.ppermute(lane_up, "row", shift_pairs(n_row, nz, 1, 2))
            lane_down = lax.ppermute(lane_down, "row", shift_pairs(n_row, nz, 1, -2))
            pieces[nz - 2 * t] = lane_up
            pieces[2 * t] = lane_down
        else:
            last_up = lax.ppermute(lane_up[..., :half], "row", shift_pairs(n_row, nz, 1, 2))
            last_down = lax.ppermute(lane_down[..., half:], "row", shift_pairs(n_row, nz, 1, -2))
            pieces[nz // 2] = jnp.concatenate([last_up, last_down], axis=-1)
    return pieces, z


def reduce_cols(value, n_col):
    ny = n_col // (X_HI * CORES)
    c = lax.axis_index("col")
    core = c % CORES
    y = (c // CORES) % ny
    x_hi = c // (CORES * ny)
    send = jnp.take(value, 1 - core, axis=2)
    keep = jnp.take(value, core, axis=2)
    value = keep + lax.ppermute(send, "col", [(p, p ^ 1) for p in range(n_col)])
    rows = value.shape[2]
    upper = value[:, :, : rows // 2]
    lower = value[:, :, rows // 2 :]
    up = shift_pairs(n_col, ny, CORES, 1)
    down = shift_pairs(n_col, ny, CORES, -1)
    acc_up = jnp.take(upper, (y - 1) % ny, axis=1)
    acc_down = jnp.take(lower, (y + 1) % ny, axis=1)
    for s in range(1, ny):
        acc_up = lax.ppermute(acc_up, "col", up) + jnp.take(upper, (y - s - 1) % ny, axis=1)
        acc_down = lax.ppermute(acc_down, "col", down) + jnp.take(lower, (y + s + 1) % ny, axis=1)
    value = jnp.concatenate([acc_up, acc_down], axis=1)
    send = jnp.take(value, 1 - x_hi, axis=0)
    keep = jnp.take(value, x_hi, axis=0)
    half = n_col // X_HI
    return keep + lax.ppermute(send, "col", [(p, (p + half) % n_col) for p in range(n_col)])


def local(anc_inv, factors_first, factors_second, lists_first, lists_second, parents, parent_link):
    n_row = lax.axis_size("row")
    n_col = lax.axis_size("col")
    local_rows, local_cols = anc_inv.shape
    n_first = factors_first.shape[0]
    n_second = factors_second.shape[0]
    members = n_first + n_second
    share_rows = factors_first.shape[1]
    panel_width = parent_link.shape[1]
    nz = n_row // X_LO
    row_anchor = lax.axis_index("row") * local_rows
    col_anchor = lax.axis_index("col") * local_cols
    out_first = tile_flags(lists_first, row_anchor, local_rows, panel_width)
    out_second = tile_flags(lists_second, row_anchor, local_rows, panel_width)
    panels = jnp.concatenate([factors_first, factors_second], axis=0)
    stacked = jnp.transpose(panels, (1, 0, 2)).reshape(share_rows, members * local_cols)
    pieces, z = gather_rows(stacked, n_row)
    col_mask = jnp.concatenate(
        [
            tile_flags(lists_first, col_anchor, local_cols, panel_width),
            tile_flags(lists_second, col_anchor, local_cols, panel_width),
        ],
        axis=0,
    )

    def apply_pieces(offsets):
        block = jnp.stack([pieces[t] for t in offsets]).reshape(
            len(offsets), X_LO, share_rows, members, local_cols
        )
        return jnp.einsum(
            "tlkmj,ij->ltkmi", block * col_mask, anc_inv, precision=highest, preferred_element_type=jnp.float32
        )

    late = [nz // 2 - 1, nz // 2, nz // 2 + 1]
    early = [t for t in range(nz) if t not in late]
    products = jnp.concatenate([apply_pieces(early), apply_pieces(late)], axis=1)
    order = early + late
    partial_value = jnp.take(products, jnp.array([order.index(t) for t in range(nz)]), axis=1)
    partial_value = jnp.roll(partial_value, z, axis=1)
    partial_value = partial_value.reshape(panel_width, members, local_rows)
    first_partial = partial_value[:, :n_first]
    chosen = jnp.take(first_partial, parents, axis=1)
    chosen_mask = jnp.take(out_first, parents, axis=0)
    coupling = jnp.einsum("cqk,qci->kci", parent_link, chosen, precision=highest)
    second_partial = partial_value[:, n_first:] - chosen_mask[None, :, :] * coupling
    combined = jnp.concatenate([first_partial, second_partial], axis=1)
    combined = combined.reshape(n_col, panel_width // n_col, members, local_rows)
    reduced = jnp.sum(lax.all_to_all(combined, "col", 0, 0, tiled=True), axis=0)
    reduced = jnp.transpose(reduced, (1, 0, 2))
    first_cols = -out_first[:, None, :] * reduced[:n_first]
    second_cols = -out_second[:, None, :] * reduced[n_first:]
    return (first_cols, second_cols)


def solution(mesh):
    in_specs = (P("row", "col"), P(None, "row", "col"), P(None, "row", "col"), P(), P(), P(), P())
    out_specs = (P(None, "col", "row"), P(None, "col", "row"))
    return jax.shard_map(local, mesh=mesh, in_specs=in_specs, out_specs=out_specs, check_vma=False)
```

```python
import jax
import jax.numpy as jnp
from jax import lax
from jax.sharding import PartitionSpec as P

high = lax.Precision.HIGH

X_LO = 2
X_HI = 2
CORES = 2


def tile_flags(block_lists, anchor, extent, tile_height):
    tile_ids = (anchor + jnp.arange(extent, dtype=jnp.int32)) // tile_height
    matches = block_lists[:, :, None] == tile_ids[None, None, :]
    return jnp.any(matches, axis=1).astype(jnp.float32)


def shift_pairs(size, inner, stride, shift):
    pairs = []
    for p in range(size):
        q = (p // stride) % inner
        target = p + (((q + shift) % inner) - q) * stride
        pairs.append((p, target))
    return pairs


def gather_rows(block, n_row):
    nz = n_row // X_LO
    r = lax.axis_index("row")
    x_lo = r // nz
    z = r % nz
    partner = lax.ppermute(block, "row", [(p, (p + nz) % n_row) for p in range(n_row)])
    pair = jnp.where(x_lo == 0, jnp.stack([block, partner]), jnp.stack([partner, block]))
    pieces = [None] * nz
    pieces[0] = pair
    steps = nz // 4
    half = pair.shape[-1] // 2
    lane_up = pair
    lane_down = pair
    for t in range(1, steps + 1):
        pieces[nz - (2 * t - 1)] = lax.ppermute(lane_up, "row", shift_pairs(n_row, nz, 1, 1))
        pieces[2 * t - 1] = lax.ppermute(lane_down, "row", shift_pairs(n_row, nz, 1, -1))
        if t < steps:
            lane_up = lax.ppermute(lane_up, "row", shift_pairs(n_row, nz, 1, 2))
            lane_down = lax.ppermute(lane_down, "row", shift_pairs(n_row, nz, 1, -2))
            pieces[nz - 2 * t] = lane_up
            pieces[2 * t] = lane_down
        else:
            last_up = lax.ppermute(lane_up[..., :half], "row", shift_pairs(n_row, nz, 1, 2))
            last_down = lax.ppermute(lane_down[..., half:], "row", shift_pairs(n_row, nz, 1, -2))
            pieces[nz // 2] = jnp.concatenate([last_up, last_down], axis=-1)
    return jnp.stack(pieces), z


def reduce_cols(value, n_col):
    ny = n_col // (X_HI * CORES)
    c = lax.axis_index("col")
    core = c % CORES
    y = (c // CORES) % ny
    x_hi = c // (CORES * ny)
    send = jnp.take(value, 1 - core, axis=2)
    keep = jnp.take(value, core, axis=2)
    value = keep + lax.ppermute(send, "col", [(p, p ^ 1) for p in range(n_col)])
    rows = value.shape[2]
    upper = value[:, :, : rows // 2]
    lower = value[:, :, rows // 2 :]
    up = shift_pairs(n_col, ny, CORES, 1)
    down = shift_pairs(n_col, ny, CORES, -1)
    acc_up = jnp.take(upper, (y - 1) % ny, axis=1)
    acc_down = jnp.take(lower, (y + 1) % ny, axis=1)
    for s in range(1, ny):
        acc_up = lax.ppermute(acc_up, "col", up) + jnp.take(upper, (y - s - 1) % ny, axis=1)
        acc_down = lax.ppermute(acc_down, "col", down) + jnp.take(lower, (y + s + 1) % ny, axis=1)
    value = jnp.concatenate([acc_up, acc_down], axis=1)
    send = jnp.take(value, 1 - x_hi, axis=0)
    keep = jnp.take(value, x_hi, axis=0)
    half = n_col // X_HI
    return keep + lax.ppermute(send, "col", [(p, (p + half) % n_col) for p in range(n_col)])


def local(anc_inv, factors_first, factors_second, lists_first, lists_second, parents, parent_link):
    n_row = lax.axis_size("row")
    n_col = lax.axis_size("col")
    local_rows, local_cols = anc_inv.shape
    n_first = factors_first.shape[0]
    n_second = factors_second.shape[0]
    members = n_first + n_second
    share_rows = factors_first.shape[1]
    panel_width = parent_link.shape[1]
    nz = n_row // X_LO
    row_anchor = lax.axis_index("row") * local_rows
    col_anchor = lax.axis_index("col") * local_cols
    out_first = tile_flags(lists_first, row_anchor, local_rows, panel_width)
    out_second = tile_flags(lists_second, row_anchor, local_rows, panel_width)
    panels = jnp.concatenate([factors_first, factors_second], axis=0)
    pieces, z = gather_rows(panels, n_row)
    col_mask = jnp.concatenate(
        [
            tile_flags(lists_first, col_anchor, local_cols, panel_width),
            tile_flags(lists_second, col_anchor, local_cols, panel_width),
        ],
        axis=0,
    )
    pieces = pieces * col_mask[None, None, :, None, :]
    partial_value = jnp.einsum(
        "tlmkj,ij->ltkmi", pieces, anc_inv, precision=high, preferred_element_type=jnp.float32
    )
    partial_value = jnp.roll(partial_value, z, axis=1)
    partial_value = partial_value.reshape(panel_width, members, local_rows)
    first_partial = partial_value[:, :n_first]
    chosen = jnp.take(first_partial, parents, axis=1)
    chosen_mask = jnp.take(out_first, parents, axis=0)
    coupling = jnp.einsum("cqk,qci->kci", parent_link, chosen, precision=high)
    second_partial = partial_value[:, n_first:] - chosen_mask[None, :, :] * coupling
    combined = jnp.concatenate([first_partial, second_partial], axis=1)
    combined = combined.reshape(n_col, panel_width // n_col, members, local_rows)
    reduced = jnp.sum(lax.all_to_all(combined, "col", 0, 0, tiled=True), axis=0)
    reduced = jnp.transpose(reduced, (1, 0, 2))
    first_cols = -out_first[:, None, :] * reduced[:n_first]
    second_cols = -out_second[:, None, :] * reduced[n_first:]
    return (first_cols, second_cols)


def solution(mesh):
    in_specs = (P("row", "col"), P(None, "row", "col"), P(None, "row", "col"), P(), P(), P(), P())
    out_specs = (P(None, "col", "row"), P(None, "col", "row"))
    return jax.shard_map(local, mesh=mesh, in_specs=in_specs, out_specs=out_specs, check_vma=False)
```

```python
import jax
import jax.numpy as jnp
from jax import lax
from jax.sharding import PartitionSpec as P

high = lax.Precision.HIGH

X_LO = 2
X_HI = 2
CORES = 2


def tile_flags(block_lists, anchor, extent, tile_height):
    tile_ids = (anchor + jnp.arange(extent, dtype=jnp.int32)) // tile_height
    matches = block_lists[:, :, None] == tile_ids[None, None, :]
    return jnp.any(matches, axis=1).astype(jnp.float32)


def shift_pairs(size, inner, stride, shift):
    pairs = []
    for p in range(size):
        q = (p // stride) % inner
        target = p + (((q + shift) % inner) - q) * stride
        pairs.append((p, target))
    return pairs


def gather_rows(block, n_row):
    nz = n_row // X_LO
    r = lax.axis_index("row")
    x_lo = r // nz
    z = r % nz
    partner = lax.ppermute(block, "row", [(p, (p + nz) % n_row) for p in range(n_row)])
    pair = jnp.where(x_lo == 0, jnp.stack([block, partner]), jnp.stack([partner, block]))
    pieces = [None] * nz
    pieces[0] = pair
    steps = nz // 4
    half = pair.shape[-1] // 2
    lane_up = pair
    lane_down = pair
    for t in range(1, steps + 1):
        pieces[nz - (2 * t - 1)] = lax.ppermute(lane_up, "row", shift_pairs(n_row, nz, 1, 1))
        pieces[2 * t - 1] = lax.ppermute(lane_down, "row", shift_pairs(n_row, nz, 1, -1))
        if t < steps:
            lane_up = lax.ppermute(lane_up, "row", shift_pairs(n_row, nz, 1, 2))
            lane_down = lax.ppermute(lane_down, "row", shift_pairs(n_row, nz, 1, -2))
            pieces[nz - 2 * t] = lane_up
            pieces[2 * t] = lane_down
        else:
            last_up = lax.ppermute(lane_up[..., :half], "row", shift_pairs(n_row, nz, 1, 2))
            last_down = lax.ppermute(lane_down[..., half:], "row", shift_pairs(n_row, nz, 1, -2))
            pieces[nz // 2] = jnp.concatenate([last_up, last_down], axis=-1)
    return jnp.stack(pieces), z


def reduce_cols(value, n_col):
    ny = n_col // (X_HI * CORES)
    c = lax.axis_index("col")
    core = c % CORES
    y = (c // CORES) % ny
    x_hi = c // (CORES * ny)
    send = jnp.take(value, 1 - core, axis=2)
    keep = jnp.take(value, core, axis=2)
    value = keep + lax.ppermute(send, "col", [(p, p ^ 1) for p in range(n_col)])
    rows = value.shape[2]
    upper = value[:, :, : rows // 2]
    lower = value[:, :, rows // 2 :]
    up = shift_pairs(n_col, ny, CORES, 1)
    down = shift_pairs(n_col, ny, CORES, -1)
    acc_up = jnp.take(upper, (y - 1) % ny, axis=1)
    acc_down = jnp.take(lower, (y + 1) % ny, axis=1)
    for s in range(1, ny):
        acc_up = lax.ppermute(acc_up, "col", up) + jnp.take(upper, (y - s - 1) % ny, axis=1)
        acc_down = lax.ppermute(acc_down, "col", down) + jnp.take(lower, (y + s + 1) % ny, axis=1)
    value = jnp.concatenate([acc_up, acc_down], axis=1)
    send = jnp.take(value, 1 - x_hi, axis=0)
    keep = jnp.take(value, x_hi, axis=0)
    half = n_col // X_HI
    return keep + lax.ppermute(send, "col", [(p, (p + half) % n_col) for p in range(n_col)])


def local(anc_inv, factors_first, factors_second, lists_first, lists_second, parents, parent_link):
    n_row = lax.axis_size("row")
    n_col = lax.axis_size("col")
    local_rows, local_cols = anc_inv.shape
    n_first = factors_first.shape[0]
    n_second = factors_second.shape[0]
    members = n_first + n_second
    share_rows = factors_first.shape[1]
    panel_width = parent_link.shape[1]
    nz = n_row // X_LO
    row_anchor = lax.axis_index("row") * local_rows
    col_anchor = lax.axis_index("col") * local_cols
    out_first = tile_flags(lists_first, row_anchor, local_rows, panel_width)
    out_second = tile_flags(lists_second, row_anchor, local_rows, panel_width)
    panels = jnp.concatenate([factors_first, factors_second], axis=0)
    stacked = jnp.transpose(panels, (1, 0, 2)).reshape(share_rows, members * local_cols)
    pieces, z = gather_rows(stacked, n_row)
    col_mask = jnp.concatenate(
        [
            tile_flags(lists_first, col_anchor, local_cols, panel_width),
            tile_flags(lists_second, col_anchor, local_cols, panel_width),
        ],
        axis=0,
    )
    pieces = pieces.reshape(nz, X_LO, share_rows, members, local_cols) * col_mask
    partial_value = jnp.einsum(
        "tlkmj,ij->ltkmi", pieces, anc_inv, precision=high, preferred_element_type=jnp.float32
    )
    partial_value = jnp.roll(partial_value, z, axis=1)
    partial_value = partial_value.reshape(panel_width, members, local_rows)
    first_partial = partial_value[:, :n_first]
    chosen = jnp.take(first_partial, parents, axis=1)
    chosen_mask = jnp.take(out_first, parents, axis=0)
    coupling = jnp.einsum("cqk,qci->kci", parent_link, chosen, precision=high)
    second_partial = partial_value[:, n_first:] - chosen_mask[None, :, :] * coupling
    combined = jnp.concatenate([first_partial, second_partial], axis=1)
    combined = combined.reshape(n_col, panel_width // n_col, members, local_rows)
    reduced = jnp.sum(lax.all_to_all(combined, "col", 0, 0, tiled=True), axis=0)
    reduced = jnp.transpose(reduced, (1, 0, 2))
    first_cols = -out_first[:, None, :] * reduced[:n_first]
    second_cols = -out_second[:, None, :] * reduced[n_first:]
    return (first_cols, second_cols)


def solution(mesh):
    in_specs = (P("row", "col"), P(None, "row", "col"), P(None, "row", "col"), P(), P(), P(), P())
    out_specs = (P(None, "col", "row"), P(None, "col", "row"))
    return jax.shard_map(local, mesh=mesh, in_specs=in_specs, out_specs=out_specs, check_vma=False)
```

```python
import jax
import jax.numpy as jnp
from jax import lax
from jax.sharding import PartitionSpec as P

high = lax.Precision.HIGH

X_LO = 2
X_HI = 2
CORES = 2


def tile_flags(block_lists, anchor, extent, tile_height):
    tile_ids = (anchor + jnp.arange(extent, dtype=jnp.int32)) // tile_height
    matches = block_lists[:, :, None] == tile_ids[None, None, :]
    return jnp.any(matches, axis=1).astype(jnp.float32)


def shift_pairs(size, inner, stride, shift):
    pairs = []
    for p in range(size):
        q = (p // stride) % inner
        target = p + (((q + shift) % inner) - q) * stride
        pairs.append((p, target))
    return pairs


def gather_rows(block, n_row):
    nz = n_row // X_LO
    r = lax.axis_index("row")
    x_lo = r // nz
    z = r % nz
    partner = lax.ppermute(block, "row", [(p, (p + nz) % n_row) for p in range(n_row)])
    pair = jnp.where(x_lo == 0, jnp.stack([block, partner]), jnp.stack([partner, block]))
    pieces = [None] * nz
    pieces[0] = pair
    steps = nz // 4
    half = pair.shape[-1] // 2
    lane_up = pair
    lane_down = pair
    for t in range(1, steps + 1):
        pieces[nz - (2 * t - 1)] = lax.ppermute(lane_up, "row", shift_pairs(n_row, nz, 1, 1))
        pieces[2 * t - 1] = lax.ppermute(lane_down, "row", shift_pairs(n_row, nz, 1, -1))
        if t < steps:
            lane_up = lax.ppermute(lane_up, "row", shift_pairs(n_row, nz, 1, 2))
            lane_down = lax.ppermute(lane_down, "row", shift_pairs(n_row, nz, 1, -2))
            pieces[nz - 2 * t] = lane_up
            pieces[2 * t] = lane_down
        else:
            last_up = lax.ppermute(lane_up[..., :half], "row", shift_pairs(n_row, nz, 1, 2))
            last_down = lax.ppermute(lane_down[..., half:], "row", shift_pairs(n_row, nz, 1, -2))
            pieces[nz // 2] = jnp.concatenate([last_up, last_down], axis=-1)
    return jnp.stack(pieces), z


def reduce_cols(value, n_col):
    ny = n_col // (X_HI * CORES)
    c = lax.axis_index("col")
    core = c % CORES
    y = (c // CORES) % ny
    x_hi = c // (CORES * ny)
    send = jnp.take(value, 1 - core, axis=2)
    keep = jnp.take(value, core, axis=2)
    value = keep + lax.ppermute(send, "col", [(p, p ^ 1) for p in range(n_col)])
    rows = value.shape[2]
    upper = value[:, :, : rows // 2]
    lower = value[:, :, rows // 2 :]
    up = shift_pairs(n_col, ny, CORES, 1)
    down = shift_pairs(n_col, ny, CORES, -1)
    acc_up = jnp.take(upper, (y - 1) % ny, axis=1)
    acc_down = jnp.take(lower, (y + 1) % ny, axis=1)
    for s in range(1, ny):
        acc_up = lax.ppermute(acc_up, "col", up) + jnp.take(upper, (y - s - 1) % ny, axis=1)
        acc_down = lax.ppermute(acc_down, "col", down) + jnp.take(lower, (y + s + 1) % ny, axis=1)
    value = jnp.concatenate([acc_up, acc_down], axis=1)
    send = jnp.take(value, 1 - x_hi, axis=0)
    keep = jnp.take(value, x_hi, axis=0)
    half = n_col // X_HI
    return keep + lax.ppermute(send, "col", [(p, (p + half) % n_col) for p in range(n_col)])


def reduce_cols_a2a(value, n_col):
    chips = n_col // CORES
    rows = value.shape[0] // n_col
    core = lax.axis_index("col") % CORES
    value = value.reshape(chips, CORES, rows, *value.shape[1:])
    partner_pairs = [(p, p ^ 1) for p in range(n_col)]
    send = jnp.take(value, 1 - core, axis=1)
    summed = jnp.take(value, core, axis=1) + lax.ppermute(send, "col", partner_pairs)
    half = rows // CORES
    summed = summed.reshape(n_col, half, *value.shape[3:])
    received = lax.all_to_all(summed, "col", 0, 0, tiled=True)
    totals = jnp.sum(received.reshape(chips, CORES, half, *value.shape[3:]), axis=0)
    own = jnp.take(totals, core, axis=0)
    other = lax.ppermute(jnp.take(totals, 1 - core, axis=0), "col", partner_pairs)
    return jnp.where(core == 0, jnp.concatenate([own, other]), jnp.concatenate([other, own]))


def local(anc_inv, factors_first, factors_second, lists_first, lists_second, parents, parent_link):
    n_row = lax.axis_size("row")
    n_col = lax.axis_size("col")
    local_rows, local_cols = anc_inv.shape
    n_first = factors_first.shape[0]
    n_second = factors_second.shape[0]
    members = n_first + n_second
    share_rows = factors_first.shape[1]
    panel_width = parent_link.shape[1]
    nz = n_row // X_LO
    row_anchor = lax.axis_index("row") * local_rows
    col_anchor = lax.axis_index("col") * local_cols
    out_first = tile_flags(lists_first, row_anchor, local_rows, panel_width)
    out_second = tile_flags(lists_second, row_anchor, local_rows, panel_width)
    panels = jnp.concatenate([factors_first, factors_second], axis=0)
    stacked = jnp.transpose(panels, (1, 0, 2)).reshape(share_rows, members * local_cols)
    pieces, z = gather_rows(stacked, n_row)
    col_mask = jnp.concatenate(
        [
            tile_flags(lists_first, col_anchor, local_cols, panel_width),
            tile_flags(lists_second, col_anchor, local_cols, panel_width),
        ],
        axis=0,
    )
    pieces = pieces.reshape(nz, X_LO, share_rows, members, local_cols) * col_mask
    partial_value = jnp.einsum(
        "tlkmj,ij->ltkmi", pieces, anc_inv, precision=high, preferred_element_type=jnp.float32
    )
    partial_value = jnp.roll(partial_value, z, axis=1)
    partial_value = partial_value.reshape(panel_width, members, local_rows)
    first_partial = partial_value[:, :n_first]
    chosen = jnp.take(first_partial, parents, axis=1)
    chosen_mask = jnp.take(out_first, parents, axis=0)
    coupling = jnp.einsum("cqk,qci->kci", parent_link, chosen, precision=high)
    second_partial = partial_value[:, n_first:] - chosen_mask[None, :, :] * coupling
    combined = jnp.concatenate([first_partial, second_partial], axis=1)
    reduced = reduce_cols_a2a(combined, n_col)
    reduced = jnp.transpose(reduced, (1, 0, 2))
    first_cols = -out_first[:, None, :] * reduced[:n_first]
    second_cols = -out_second[:, None, :] * reduced[n_first:]
    return (first_cols, second_cols)


def solution(mesh):
    in_specs = (P("row", "col"), P(None, "row", "col"), P(None, "row", "col"), P(), P(), P(), P())
    out_specs = (P(None, "col", "row"), P(None, "col", "row"))
    return jax.shard_map(local, mesh=mesh, in_specs=in_specs, out_specs=out_specs, check_vma=False)
```

```python
import jax
import jax.numpy as jnp
from jax import lax
from jax.sharding import PartitionSpec as P

high = lax.Precision.HIGH

X_LO = 2
X_HI = 2
CORES = 2


def tile_flags(block_lists, anchor, extent, tile_height):
    tile_ids = (anchor + jnp.arange(extent, dtype=jnp.int32)) // tile_height
    matches = block_lists[:, :, None] == tile_ids[None, None, :]
    return jnp.any(matches, axis=1).astype(jnp.float32)


def shift_pairs(size, inner, stride, shift):
    pairs = []
    for p in range(size):
        q = (p // stride) % inner
        target = p + (((q + shift) % inner) - q) * stride
        pairs.append((p, target))
    return pairs


def gather_rows(block, n_row):
    nz = n_row // X_LO
    r = lax.axis_index("row")
    x_lo = r // nz
    z = r % nz
    partner = lax.ppermute(block, "row", [(p, (p + nz) % n_row) for p in range(n_row)])
    pair = jnp.where(x_lo == 0, jnp.stack([block, partner]), jnp.stack([partner, block]))
    pieces = [None] * nz
    pieces[0] = pair
    steps = nz // 4
    half = pair.shape[-1] // 2
    lane_up = pair
    lane_down = pair
    for t in range(1, steps + 1):
        pieces[nz - (2 * t - 1)] = lax.ppermute(lane_up, "row", shift_pairs(n_row, nz, 1, 1))
        pieces[2 * t - 1] = lax.ppermute(lane_down, "row", shift_pairs(n_row, nz, 1, -1))
        if t < steps:
            lane_up = lax.ppermute(lane_up, "row", shift_pairs(n_row, nz, 1, 2))
            lane_down = lax.ppermute(lane_down, "row", shift_pairs(n_row, nz, 1, -2))
            pieces[nz - 2 * t] = lane_up
            pieces[2 * t] = lane_down
        else:
            last_up = lax.ppermute(lane_up[..., :half], "row", shift_pairs(n_row, nz, 1, 2))
            last_down = lax.ppermute(lane_down[..., half:], "row", shift_pairs(n_row, nz, 1, -2))
            pieces[nz // 2] = jnp.concatenate([last_up, last_down], axis=-1)
    return jnp.stack(pieces), z


def reduce_cols(value, n_col):
    ny = n_col // (X_HI * CORES)
    c = lax.axis_index("col")
    core = c % CORES
    y = (c // CORES) % ny
    x_hi = c // (CORES * ny)
    send = jnp.take(value, 1 - core, axis=2)
    keep = jnp.take(value, core, axis=2)
    value = keep + lax.ppermute(send, "col", [(p, p ^ 1) for p in range(n_col)])
    rows = value.shape[2]
    upper = value[:, :, : rows // 2]
    lower = value[:, :, rows // 2 :]
    up = shift_pairs(n_col, ny, CORES, 1)
    down = shift_pairs(n_col, ny, CORES, -1)
    acc_up = jnp.take(upper, (y - 1) % ny, axis=1)
    acc_down = jnp.take(lower, (y + 1) % ny, axis=1)
    for s in range(1, ny):
        acc_up = lax.ppermute(acc_up, "col", up) + jnp.take(upper, (y - s - 1) % ny, axis=1)
        acc_down = lax.ppermute(acc_down, "col", down) + jnp.take(lower, (y + s + 1) % ny, axis=1)
    value = jnp.concatenate([acc_up, acc_down], axis=1)
    send = jnp.take(value, 1 - x_hi, axis=0)
    keep = jnp.take(value, x_hi, axis=0)
    half = n_col // X_HI
    return keep + lax.ppermute(send, "col", [(p, (p + half) % n_col) for p in range(n_col)])


def reduce_cols_a2a(value, n_col):
    chips = n_col // CORES
    rows = value.shape[0] // n_col
    core = lax.axis_index("col") % CORES
    value = value.reshape(chips, CORES, rows, *value.shape[1:])
    partner_pairs = [(p, p ^ 1) for p in range(n_col)]
    send = jnp.take(value, 1 - core, axis=1)
    summed = jnp.take(value, core, axis=1) + lax.ppermute(send, "col", partner_pairs)
    groups = [list(range(e, n_col, CORES)) for e in range(CORES)]
    received = lax.all_to_all(summed, "col", 0, 0, tiled=True, axis_index_groups=groups)
    return jnp.sum(received, axis=0)


def local(anc_inv, factors_first, factors_second, lists_first, lists_second, parents, parent_link):
    n_row = lax.axis_size("row")
    n_col = lax.axis_size("col")
    local_rows, local_cols = anc_inv.shape
    n_first = factors_first.shape[0]
    n_second = factors_second.shape[0]
    members = n_first + n_second
    share_rows = factors_first.shape[1]
    panel_width = parent_link.shape[1]
    nz = n_row // X_LO
    row_anchor = lax.axis_index("row") * local_rows
    col_anchor = lax.axis_index("col") * local_cols
    out_first = tile_flags(lists_first, row_anchor, local_rows, panel_width)
    out_second = tile_flags(lists_second, row_anchor, local_rows, panel_width)
    panels = jnp.concatenate([factors_first, factors_second], axis=0)
    stacked = jnp.transpose(panels, (1, 0, 2)).reshape(share_rows, members * local_cols)
    pieces, z = gather_rows(stacked, n_row)
    col_mask = jnp.concatenate(
        [
            tile_flags(lists_first, col_anchor, local_cols, panel_width),
            tile_flags(lists_second, col_anchor, local_cols, panel_width),
        ],
        axis=0,
    )
    pieces = pieces.reshape(nz, X_LO, share_rows, members, local_cols) * col_mask
    partial_value = jnp.einsum(
        "tlkmj,ij->ltkmi", pieces, anc_inv, precision=high, preferred_element_type=jnp.float32
    )
    partial_value = jnp.roll(partial_value, z, axis=1)
    partial_value = partial_value.reshape(panel_width, members, local_rows)
    first_partial = partial_value[:, :n_first]
    chosen = jnp.take(first_partial, parents, axis=1)
    chosen_mask = jnp.take(out_first, parents, axis=0)
    coupling = jnp.einsum("cqk,qci->kci", parent_link, chosen, precision=high)
    second_partial = partial_value[:, n_first:] - chosen_mask[None, :, :] * coupling
    combined = jnp.concatenate([first_partial, second_partial], axis=1)
    reduced = reduce_cols_a2a(combined, n_col)
    reduced = jnp.transpose(reduced, (1, 0, 2))
    first_cols = -out_first[:, None, :] * reduced[:n_first]
    second_cols = -out_second[:, None, :] * reduced[n_first:]
    return (first_cols, second_cols)


def solution(mesh):
    in_specs = (P("row", "col"), P(None, "row", "col"), P(None, "row", "col"), P(), P(), P(), P())
    out_specs = (P(None, "col", "row"), P(None, "col", "row"))
    return jax.shard_map(local, mesh=mesh, in_specs=in_specs, out_specs=out_specs, check_vma=False)
```

```python
import jax
import jax.numpy as jnp
from jax import lax
from jax.sharding import PartitionSpec as P

high = lax.Precision.HIGH

X_LO = 2
X_HI = 2
CORES = 2


def tile_flags(block_lists, anchor, extent, tile_height):
    tile_ids = (anchor + jnp.arange(extent, dtype=jnp.int32)) // tile_height
    matches = block_lists[:, :, None] == tile_ids[None, None, :]
    return jnp.any(matches, axis=1).astype(jnp.float32)


def shift_pairs(size, inner, stride, shift):
    pairs = []
    for p in range(size):
        q = (p // stride) % inner
        target = p + (((q + shift) % inner) - q) * stride
        pairs.append((p, target))
    return pairs


def gather_rows(block, n_row):
    nz = n_row // X_LO
    r = lax.axis_index("row")
    x_lo = r // nz
    z = r % nz
    partner = lax.ppermute(block, "row", [(p, (p + nz) % n_row) for p in range(n_row)])
    pair = jnp.where(x_lo == 0, jnp.stack([block, partner]), jnp.stack([partner, block]))
    pieces = [None] * nz
    pieces[0] = pair
    steps = nz // 4
    lane_up = pair
    lane_down = pair
    for t in range(1, steps + 1):
        pieces[nz - (2 * t - 1)] = lax.ppermute(lane_up, "row", shift_pairs(n_row, nz, 1, 1))
        pieces[2 * t - 1] = lax.ppermute(lane_down, "row", shift_pairs(n_row, nz, 1, -1))
        lane_up = lax.ppermute(lane_up, "row", shift_pairs(n_row, nz, 1, 2))
        pieces[nz - 2 * t] = lane_up
        if t < steps:
            lane_down = lax.ppermute(lane_down, "row", shift_pairs(n_row, nz, 1, -2))
            pieces[2 * t] = lane_down
    return jnp.stack(pieces), z


def reduce_cols(value, n_col):
    ny = n_col // (X_HI * CORES)
    c = lax.axis_index("col")
    core = c % CORES
    y = (c // CORES) % ny
    x_hi = c // (CORES * ny)
    send = jnp.take(value, 1 - core, axis=2)
    keep = jnp.take(value, core, axis=2)
    value = keep + lax.ppermute(send, "col", [(p, p ^ 1) for p in range(n_col)])
    rows = value.shape[2]
    upper = value[:, :, : rows // 2]
    lower = value[:, :, rows // 2 :]
    up = shift_pairs(n_col, ny, CORES, 1)
    down = shift_pairs(n_col, ny, CORES, -1)
    acc_up = jnp.take(upper, (y - 1) % ny, axis=1)
    acc_down = jnp.take(lower, (y + 1) % ny, axis=1)
    for s in range(1, ny):
        acc_up = lax.ppermute(acc_up, "col", up) + jnp.take(upper, (y - s - 1) % ny, axis=1)
        acc_down = lax.ppermute(acc_down, "col", down) + jnp.take(lower, (y + s + 1) % ny, axis=1)
    value = jnp.concatenate([acc_up, acc_down], axis=1)
    send = jnp.take(value, 1 - x_hi, axis=0)
    keep = jnp.take(value, x_hi, axis=0)
    half = n_col // X_HI
    return keep + lax.ppermute(send, "col", [(p, (p + half) % n_col) for p in range(n_col)])


def reduce_cols_a2a(value, n_col):
    chips = n_col // CORES
    rows = value.shape[0] // n_col
    core = lax.axis_index("col") % CORES
    value = value.reshape(chips, CORES, rows, *value.shape[1:])
    partner_pairs = [(p, p ^ 1) for p in range(n_col)]
    send = jnp.take(value, 1 - core, axis=1)
    summed = jnp.take(value, core, axis=1) + lax.ppermute(send, "col", partner_pairs)
    groups = [list(range(e, n_col, CORES)) for e in range(CORES)]
    received = lax.all_to_all(summed, "col", 0, 0, tiled=True, axis_index_groups=groups)
    return jnp.sum(received, axis=0)


def local(anc_inv, factors_first, factors_second, lists_first, lists_second, parents, parent_link):
    n_row = lax.axis_size("row")
    n_col = lax.axis_size("col")
    local_rows, local_cols = anc_inv.shape
    n_first = factors_first.shape[0]
    n_second = factors_second.shape[0]
    members = n_first + n_second
    share_rows = factors_first.shape[1]
    panel_width = parent_link.shape[1]
    nz = n_row // X_LO
    row_anchor = lax.axis_index("row") * local_rows
    col_anchor = lax.axis_index("col") * local_cols
    out_first = tile_flags(lists_first, row_anchor, local_rows, panel_width)
    out_second = tile_flags(lists_second, row_anchor, local_rows, panel_width)
    panels = jnp.concatenate([factors_first, factors_second], axis=0)
    stacked = jnp.transpose(panels, (1, 0, 2)).reshape(share_rows, members * local_cols)
    pieces, z = gather_rows(stacked, n_row)
    col_mask = jnp.concatenate(
        [
            tile_flags(lists_first, col_anchor, local_cols, panel_width),
            tile_flags(lists_second, col_anchor, local_cols, panel_width),
        ],
        axis=0,
    )
    pieces = pieces.reshape(nz, X_LO, share_rows, members, local_cols) * col_mask
    partial_value = jnp.einsum(
        "tlkmj,ij->ltkmi", pieces, anc_inv, precision=high, preferred_element_type=jnp.float32
    )
    partial_value = jnp.roll(partial_value, z, axis=1)
    partial_value = partial_value.reshape(panel_width, members, local_rows)
    first_partial = partial_value[:, :n_first]
    chosen = jnp.take(first_partial, parents, axis=1)
    chosen_mask = jnp.take(out_first, parents, axis=0)
    coupling = jnp.einsum("cqk,qci->kci", parent_link, chosen, precision=high)
    second_partial = partial_value[:, n_first:] - chosen_mask[None, :, :] * coupling
    combined = jnp.concatenate([first_partial, second_partial], axis=1)
    reduced = reduce_cols_a2a(combined, n_col)
    reduced = jnp.transpose(reduced, (1, 0, 2))
    first_cols = -out_first[:, None, :] * reduced[:n_first]
    second_cols = -out_second[:, None, :] * reduced[n_first:]
    return (first_cols, second_cols)


def solution(mesh):
    in_specs = (P("row", "col"), P(None, "row", "col"), P(None, "row", "col"), P(), P(), P(), P())
    out_specs = (P(None, "col", "row"), P(None, "col", "row"))
    return jax.shard_map(local, mesh=mesh, in_specs=in_specs, out_specs=out_specs, check_vma=False)
```

```python
import jax
import jax.numpy as jnp
from jax import lax
from jax.sharding import PartitionSpec as P

high = lax.Precision.HIGH

X_LO = 2
X_HI = 2
CORES = 2


def tile_flags(block_lists, anchor, extent, tile_height):
    tile_ids = (anchor + jnp.arange(extent, dtype=jnp.int32)) // tile_height
    matches = block_lists[:, :, None] == tile_ids[None, None, :]
    return jnp.any(matches, axis=1).astype(jnp.float32)


def shift_pairs(size, inner, stride, shift):
    pairs = []
    for p in range(size):
        q = (p // stride) % inner
        target = p + (((q + shift) % inner) - q) * stride
        pairs.append((p, target))
    return pairs


def gather_rows(block, n_row):
    nz = n_row // X_LO
    r = lax.axis_index("row")
    x_lo = r // nz
    z = r % nz
    partner = lax.ppermute(block, "row", [(p, (p + nz) % n_row) for p in range(n_row)])
    pair = jnp.where(x_lo == 0, jnp.stack([block, partner]), jnp.stack([partner, block]))
    pieces = [None] * nz
    pieces[0] = pair
    steps = nz // 4
    half = pair.shape[-1] // 2
    lane_up = pair
    lane_down = pair
    for t in range(1, steps + 1):
        pieces[nz - (2 * t - 1)] = lax.ppermute(lane_up, "row", shift_pairs(n_row, nz, 1, 1))
        pieces[2 * t - 1] = lax.ppermute(lane_down, "row", shift_pairs(n_row, nz, 1, -1))
        if t < steps:
            lane_up = lax.ppermute(lane_up, "row", shift_pairs(n_row, nz, 1, 2))
            lane_down = lax.ppermute(lane_down, "row", shift_pairs(n_row, nz, 1, -2))
            pieces[nz - 2 * t] = lane_up
            pieces[2 * t] = lane_down
        else:
            last_up = lax.ppermute(lane_up[..., :half], "row", shift_pairs(n_row, nz, 1, 2))
            last_down = lax.ppermute(lane_down[..., half:], "row", shift_pairs(n_row, nz, 1, -2))
            pieces[nz // 2] = jnp.concatenate([last_up, last_down], axis=-1)
    gathered = jnp.zeros((nz,) + pair.shape, pair.dtype)
    for t, piece in enumerate(pieces):
        gathered = lax.dynamic_update_index_in_dim(gathered, piece, (z + t) % nz, 0)
    return gathered


def reduce_cols(value, n_col):
    ny = n_col // (X_HI * CORES)
    c = lax.axis_index("col")
    core = c % CORES
    y = (c // CORES) % ny
    x_hi = c // (CORES * ny)
    send = jnp.take(value, 1 - core, axis=2)
    keep = jnp.take(value, core, axis=2)
    value = keep + lax.ppermute(send, "col", [(p, p ^ 1) for p in range(n_col)])
    rows = value.shape[2]
    upper = value[:, :, : rows // 2]
    lower = value[:, :, rows // 2 :]
    up = shift_pairs(n_col, ny, CORES, 1)
    down = shift_pairs(n_col, ny, CORES, -1)
    acc_up = jnp.take(upper, (y - 1) % ny, axis=1)
    acc_down = jnp.take(lower, (y + 1) % ny, axis=1)
    for s in range(1, ny):
        acc_up = lax.ppermute(acc_up, "col", up) + jnp.take(upper, (y - s - 1) % ny, axis=1)
        acc_down = lax.ppermute(acc_down, "col", down) + jnp.take(lower, (y + s + 1) % ny, axis=1)
    value = jnp.concatenate([acc_up, acc_down], axis=1)
    send = jnp.take(value, 1 - x_hi, axis=0)
    keep = jnp.take(value, x_hi, axis=0)
    half = n_col // X_HI
    return keep + lax.ppermute(send, "col", [(p, (p + half) % n_col) for p in range(n_col)])


def reduce_cols_a2a(value, n_col):
    chips = n_col // CORES
    rows = value.shape[0] // n_col
    core = lax.axis_index("col") % CORES
    value = value.reshape(chips, CORES, rows, *value.shape[1:])
    partner_pairs = [(p, p ^ 1) for p in range(n_col)]
    send = jnp.take(value, 1 - core, axis=1)
    summed = jnp.take(value, core, axis=1) + lax.ppermute(send, "col", partner_pairs)
    groups = [list(range(e, n_col, CORES)) for e in range(CORES)]
    received = lax.all_to_all(summed, "col", 0, 0, tiled=True, axis_index_groups=groups)
    return jnp.sum(received, axis=0)


def local(anc_inv, factors_first, factors_second, lists_first, lists_second, parents, parent_link):
    n_row = lax.axis_size("row")
    n_col = lax.axis_size("col")
    local_rows, local_cols = anc_inv.shape
    n_first = factors_first.shape[0]
    n_second = factors_second.shape[0]
    members = n_first + n_second
    share_rows = factors_first.shape[1]
    panel_width = parent_link.shape[1]
    nz = n_row // X_LO
    row_anchor = lax.axis_index("row") * local_rows
    col_anchor = lax.axis_index("col") * local_cols
    out_first = tile_flags(lists_first, row_anchor, local_rows, panel_width)
    out_second = tile_flags(lists_second, row_anchor, local_rows, panel_width)
    panels = jnp.concatenate([factors_first, factors_second], axis=0)
    stacked = jnp.transpose(panels, (1, 0, 2)).reshape(share_rows, members * local_cols)
    pieces = gather_rows(stacked, n_row)
    col_mask = jnp.concatenate(
        [
            tile_flags(lists_first, col_anchor, local_cols, panel_width),
            tile_flags(lists_second, col_anchor, local_cols, panel_width),
        ],
        axis=0,
    )
    pieces = pieces.reshape(nz, X_LO, share_rows, members, local_cols) * col_mask
    partial_value = jnp.einsum(
        "tlkmj,ij->ltkmi", pieces, anc_inv, precision=high, preferred_element_type=jnp.float32
    )
    partial_value = partial_value.reshape(panel_width, members, local_rows)
    first_partial = partial_value[:, :n_first]
    chosen = jnp.take(first_partial, parents, axis=1)
    chosen_mask = jnp.take(out_first, parents, axis=0)
    coupling = jnp.einsum("cqk,qci->kci", parent_link, chosen, precision=high)
    second_partial = partial_value[:, n_first:] - chosen_mask[None, :, :] * coupling
    combined = jnp.concatenate([first_partial, second_partial], axis=1)
    reduced = reduce_cols_a2a(combined, n_col)
    reduced = jnp.transpose(reduced, (1, 0, 2))
    first_cols = -out_first[:, None, :] * reduced[:n_first]
    second_cols = -out_second[:, None, :] * reduced[n_first:]
    return (first_cols, second_cols)


def solution(mesh):
    in_specs = (P("row", "col"), P(None, "row", "col"), P(None, "row", "col"), P(), P(), P(), P())
    out_specs = (P(None, "col", "row"), P(None, "col", "row"))
    return jax.shard_map(local, mesh=mesh, in_specs=in_specs, out_specs=out_specs, check_vma=False)
```

```python
import jax
import jax.numpy as jnp
from jax import lax
from jax.sharding import PartitionSpec as P

high = lax.Precision.HIGH

X_LO = 2
X_HI = 2
CORES = 2


def tile_flags(block_lists, anchor, extent, tile_height):
    tile_ids = (anchor + jnp.arange(extent, dtype=jnp.int32)) // tile_height
    matches = block_lists[:, :, None] == tile_ids[None, None, :]
    return jnp.any(matches, axis=1).astype(jnp.float32)


def shift_pairs(size, inner, stride, shift):
    pairs = []
    for p in range(size):
        q = (p // stride) % inner
        target = p + (((q + shift) % inner) - q) * stride
        pairs.append((p, target))
    return pairs


def gather_rows(block, n_row):
    nz = n_row // X_LO
    r = lax.axis_index("row")
    x_lo = r // nz
    z = r % nz
    partner = lax.ppermute(block, "row", [(p, (p + nz) % n_row) for p in range(n_row)])
    pair = jnp.stack([block, partner])
    pieces = [None] * nz
    pieces[0] = pair
    steps = nz // 4
    half = pair.shape[-1] // 2
    lane_up = pair
    lane_down = pair
    for t in range(1, steps + 1):
        pieces[nz - (2 * t - 1)] = lax.ppermute(lane_up, "row", shift_pairs(n_row, nz, 1, 1))
        pieces[2 * t - 1] = lax.ppermute(lane_down, "row", shift_pairs(n_row, nz, 1, -1))
        if t < steps:
            lane_up = lax.ppermute(lane_up, "row", shift_pairs(n_row, nz, 1, 2))
            lane_down = lax.ppermute(lane_down, "row", shift_pairs(n_row, nz, 1, -2))
            pieces[nz - 2 * t] = lane_up
            pieces[2 * t] = lane_down
        else:
            last_up = lax.ppermute(lane_up[..., :half], "row", shift_pairs(n_row, nz, 1, 2))
            last_down = lax.ppermute(lane_down[..., half:], "row", shift_pairs(n_row, nz, 1, -2))
            pieces[nz // 2] = jnp.concatenate([last_up, last_down], axis=-1)
    return jnp.stack(pieces), z, x_lo


def reduce_cols(value, n_col):
    ny = n_col // (X_HI * CORES)
    c = lax.axis_index("col")
    core = c % CORES
    y = (c // CORES) % ny
    x_hi = c // (CORES * ny)
    send = jnp.take(value, 1 - core, axis=2)
    keep = jnp.take(value, core, axis=2)
    value = keep + lax.ppermute(send, "col", [(p, p ^ 1) for p in range(n_col)])
    rows = value.shape[2]
    upper = value[:, :, : rows // 2]
    lower = value[:, :, rows // 2 :]
    up = shift_pairs(n_col, ny, CORES, 1)
    down = shift_pairs(n_col, ny, CORES, -1)
    acc_up = jnp.take(upper, (y - 1) % ny, axis=1)
    acc_down = jnp.take(lower, (y + 1) % ny, axis=1)
    for s in range(1, ny):
        acc_up = lax.ppermute(acc_up, "col", up) + jnp.take(upper, (y - s - 1) % ny, axis=1)
        acc_down = lax.ppermute(acc_down, "col", down) + jnp.take(lower, (y + s + 1) % ny, axis=1)
    value = jnp.concatenate([acc_up, acc_down], axis=1)
    send = jnp.take(value, 1 - x_hi, axis=0)
    keep = jnp.take(value, x_hi, axis=0)
    half = n_col // X_HI
    return keep + lax.ppermute(send, "col", [(p, (p + half) % n_col) for p in range(n_col)])


def reduce_cols_a2a(value, n_col):
    chips = n_col // CORES
    rows = value.shape[0] // n_col
    core = lax.axis_index("col") % CORES
    value = value.reshape(chips, CORES, rows, *value.shape[1:])
    partner_pairs = [(p, p ^ 1) for p in range(n_col)]
    send = jnp.take(value, 1 - core, axis=1)
    summed = jnp.take(value, core, axis=1) + lax.ppermute(send, "col", partner_pairs)
    groups = [list(range(e, n_col, CORES)) for e in range(CORES)]
    received = lax.all_to_all(summed, "col", 0, 0, tiled=True, axis_index_groups=groups)
    return jnp.sum(received, axis=0)


def local(anc_inv, factors_first, factors_second, lists_first, lists_second, parents, parent_link):
    n_row = lax.axis_size("row")
    n_col = lax.axis_size("col")
    local_rows, local_cols = anc_inv.shape
    n_first = factors_first.shape[0]
    n_second = factors_second.shape[0]
    members = n_first + n_second
    share_rows = factors_first.shape[1]
    panel_width = parent_link.shape[1]
    nz = n_row // X_LO
    row_anchor = lax.axis_index("row") * local_rows
    col_anchor = lax.axis_index("col") * local_cols
    out_first = tile_flags(lists_first, row_anchor, local_rows, panel_width)
    out_second = tile_flags(lists_second, row_anchor, local_rows, panel_width)
    panels = jnp.concatenate([factors_first, factors_second], axis=0)
    stacked = jnp.transpose(panels, (1, 0, 2)).reshape(share_rows, members * local_cols)
    pieces, z, x_lo = gather_rows(stacked, n_row)
    col_mask = jnp.concatenate(
        [
            tile_flags(lists_first, col_anchor, local_cols, panel_width),
            tile_flags(lists_second, col_anchor, local_cols, panel_width),
        ],
        axis=0,
    )
    pieces = pieces.reshape(nz, X_LO, share_rows, members, local_cols) * col_mask
    partial_value = jnp.einsum(
        "tlkmj,ij->ltkmi", pieces, anc_inv, precision=high, preferred_element_type=jnp.float32
    )
    source = jnp.arange(X_LO * nz)
    slot = (source // nz) ^ x_lo
    offset = (source % nz - z) % nz
    partial_value = partial_value.reshape(X_LO * nz, *partial_value.shape[2:])
    partial_value = jnp.take(partial_value, slot * nz + offset, axis=0)
    partial_value = partial_value.reshape(panel_width, members, local_rows)
    first_partial = partial_value[:, :n_first]
    chosen = jnp.take(first_partial, parents, axis=1)
    chosen_mask = jnp.take(out_first, parents, axis=0)
    coupling = jnp.einsum("cqk,qci->kci", parent_link, chosen, precision=high)
    second_partial = partial_value[:, n_first:] - chosen_mask[None, :, :] * coupling
    combined = jnp.concatenate([first_partial, second_partial], axis=1)
    reduced = reduce_cols_a2a(combined, n_col)
    reduced = jnp.transpose(reduced, (1, 0, 2))
    first_cols = -out_first[:, None, :] * reduced[:n_first]
    second_cols = -out_second[:, None, :] * reduced[n_first:]
    return (first_cols, second_cols)


def solution(mesh):
    in_specs = (P("row", "col"), P(None, "row", "col"), P(None, "row", "col"), P(), P(), P(), P())
    out_specs = (P(None, "col", "row"), P(None, "col", "row"))
    return jax.shard_map(local, mesh=mesh, in_specs=in_specs, out_specs=out_specs, check_vma=False)
```

```python
import jax
import jax.numpy as jnp
from jax import lax
from jax.sharding import PartitionSpec as P

high = lax.Precision.HIGH

X_LO = 2
X_HI = 2
CORES = 2


def tile_flags(block_lists, anchor, extent, tile_height):
    tile_ids = (anchor + jnp.arange(extent, dtype=jnp.int32)) // tile_height
    matches = block_lists[:, :, None] == tile_ids[None, None, :]
    return jnp.any(matches, axis=1).astype(jnp.float32)


def shift_pairs(size, inner, stride, shift):
    pairs = []
    for p in range(size):
        q = (p // stride) % inner
        target = p + (((q + shift) % inner) - q) * stride
        pairs.append((p, target))
    return pairs


def gather_rows(block, n_row):
    nz = n_row // X_LO
    r = lax.axis_index("row")
    x_lo = r // nz
    z = r % nz
    partner = lax.ppermute(block, "row", [(p, (p + nz) % n_row) for p in range(n_row)])
    pair = jnp.where(x_lo == 0, jnp.stack([block, partner]), jnp.stack([partner, block]))
    pieces = [None] * nz
    pieces[0] = pair
    steps = nz // 4
    half = pair.shape[-1] // 2
    lane_up = pair
    lane_down = pair
    for t in range(1, steps + 1):
        pieces[nz - (2 * t - 1)] = lax.ppermute(lane_up, "row", shift_pairs(n_row, nz, 1, 1))
        pieces[2 * t - 1] = lax.ppermute(lane_down, "row", shift_pairs(n_row, nz, 1, -1))
        if t < steps:
            lane_up = lax.ppermute(lane_up, "row", shift_pairs(n_row, nz, 1, 2))
            lane_down = lax.ppermute(lane_down, "row", shift_pairs(n_row, nz, 1, -2))
            pieces[nz - 2 * t] = lane_up
            pieces[2 * t] = lane_down
        else:
            last_up = lax.ppermute(lane_up[..., :half], "row", shift_pairs(n_row, nz, 1, 2))
            last_down = lax.ppermute(lane_down[..., half:], "row", shift_pairs(n_row, nz, 1, -2))
            pieces[nz // 2] = jnp.concatenate([last_up, last_down], axis=-1)
    return jnp.stack(pieces), z


def reduce_cols(value, n_col):
    ny = n_col // (X_HI * CORES)
    c = lax.axis_index("col")
    core = c % CORES
    y = (c // CORES) % ny
    x_hi = c // (CORES * ny)
    send = jnp.take(value, 1 - core, axis=2)
    keep = jnp.take(value, core, axis=2)
    value = keep + lax.ppermute(send, "col", [(p, p ^ 1) for p in range(n_col)])
    rows = value.shape[2]
    upper = value[:, :, : rows // 2]
    lower = value[:, :, rows // 2 :]
    up = shift_pairs(n_col, ny, CORES, 1)
    down = shift_pairs(n_col, ny, CORES, -1)
    acc_up = jnp.take(upper, (y - 1) % ny, axis=1)
    acc_down = jnp.take(lower, (y + 1) % ny, axis=1)
    for s in range(1, ny):
        acc_up = lax.ppermute(acc_up, "col", up) + jnp.take(upper, (y - s - 1) % ny, axis=1)
        acc_down = lax.ppermute(acc_down, "col", down) + jnp.take(lower, (y + s + 1) % ny, axis=1)
    value = jnp.concatenate([acc_up, acc_down], axis=1)
    send = jnp.take(value, 1 - x_hi, axis=0)
    keep = jnp.take(value, x_hi, axis=0)
    half = n_col // X_HI
    return keep + lax.ppermute(send, "col", [(p, (p + half) % n_col) for p in range(n_col)])


def reduce_cols_a2a(value, n_col):
    chips = n_col // CORES
    rows = value.shape[0] // n_col
    core = lax.axis_index("col") % CORES
    value = value.reshape(chips, CORES, rows, *value.shape[1:])
    partner_pairs = [(p, p ^ 1) for p in range(n_col)]
    send = jnp.take(value, 1 - core, axis=1)
    summed = jnp.take(value, core, axis=1) + lax.ppermute(send, "col", partner_pairs)
    groups = [list(range(e, n_col, CORES)) for e in range(CORES)]
    received = lax.all_to_all(summed, "col", 0, 0, tiled=True, axis_index_groups=groups)
    return jnp.sum(received, axis=0)


def local(anc_inv, factors_first, factors_second, lists_first, lists_second, parents, parent_link):
    n_row = lax.axis_size("row")
    n_col = lax.axis_size("col")
    local_rows, local_cols = anc_inv.shape
    n_first = factors_first.shape[0]
    n_second = factors_second.shape[0]
    members = n_first + n_second
    share_rows = factors_first.shape[1]
    panel_width = parent_link.shape[1]
    nz = n_row // X_LO
    row_anchor = lax.axis_index("row") * local_rows
    col_anchor = lax.axis_index("col") * local_cols
    out_first = tile_flags(lists_first, row_anchor, local_rows, panel_width)
    out_second = tile_flags(lists_second, row_anchor, local_rows, panel_width)
    panels = jnp.concatenate([factors_first, factors_second], axis=0)
    stacked = jnp.transpose(panels, (1, 0, 2)).reshape(share_rows, members * local_cols)
    pieces, z = gather_rows(stacked, n_row)
    col_mask = jnp.concatenate(
        [
            tile_flags(lists_first, col_anchor, local_cols, panel_width),
            tile_flags(lists_second, col_anchor, local_cols, panel_width),
        ],
        axis=0,
    )
    pieces = pieces.reshape(nz, X_LO, share_rows, members, local_cols) * col_mask
    partial_value = jnp.einsum(
        "tlkmj,ij->ltkmi", pieces, anc_inv, precision=high, preferred_element_type=jnp.float32
    )
    partial_value = jnp.roll(partial_value, z, axis=1)
    partial_value = partial_value.reshape(panel_width, members, local_rows)
    first_partial = partial_value[:, :n_first]
    chosen = jnp.take(first_partial, parents, axis=1)
    chosen_mask = jnp.take(out_first, parents, axis=0)
    coupling = jnp.einsum("cqk,qci->kci", parent_link, chosen, precision=high)
    second_partial = partial_value[:, n_first:] - chosen_mask[None, :, :] * coupling
    combined = jnp.concatenate([first_partial, second_partial], axis=1)
    reduced = reduce_cols_a2a(combined, n_col)
    reduced = jnp.transpose(reduced, (1, 0, 2))
    signed = -jnp.concatenate([out_first, out_second], axis=0)[:, None, :] * reduced
    first_cols = signed[:n_first]
    second_cols = signed[n_first:]
    return (first_cols, second_cols)


def solution(mesh):
    in_specs = (P("row", "col"), P(None, "row", "col"), P(None, "row", "col"), P(), P(), P(), P())
    out_specs = (P(None, "col", "row"), P(None, "col", "row"))
    return jax.shard_map(local, mesh=mesh, in_specs=in_specs, out_specs=out_specs, check_vma=False)
```

```python
import jax
import jax.numpy as jnp
from jax import lax
from jax.sharding import PartitionSpec as P

high = lax.Precision.HIGH

X_LO = 2
X_HI = 2
CORES = 2


def tile_flags(block_lists, anchor, extent, tile_height):
    tile_ids = (anchor + jnp.arange(extent, dtype=jnp.int32)) // tile_height
    matches = block_lists[:, :, None] == tile_ids[None, None, :]
    return jnp.any(matches, axis=1).astype(jnp.float32)


def shift_pairs(size, inner, stride, shift):
    pairs = []
    for p in range(size):
        q = (p // stride) % inner
        target = p + (((q + shift) % inner) - q) * stride
        pairs.append((p, target))
    return pairs


def gather_rows(block, n_row):
    nz = n_row // X_LO
    r = lax.axis_index("row")
    x_lo = r // nz
    z = r % nz
    partner = lax.ppermute(block, "row", [(p, (p + nz) % n_row) for p in range(n_row)])
    pair = jnp.where(x_lo == 0, jnp.stack([block, partner]), jnp.stack([partner, block]))
    pieces = [None] * nz
    pieces[0] = pair
    steps = nz // 4
    half = pair.shape[-1] // 2
    lane_up = pair
    lane_down = pair
    for t in range(1, steps + 1):
        pieces[nz - (2 * t - 1)] = lax.ppermute(lane_up, "row", shift_pairs(n_row, nz, 1, 1))
        pieces[2 * t - 1] = lax.ppermute(lane_down, "row", shift_pairs(n_row, nz, 1, -1))
        if t < steps:
            lane_up = lax.ppermute(lane_up, "row", shift_pairs(n_row, nz, 1, 2))
            lane_down = lax.ppermute(lane_down, "row", shift_pairs(n_row, nz, 1, -2))
            pieces[nz - 2 * t] = lane_up
            pieces[2 * t] = lane_down
        else:
            last_up = lax.ppermute(lane_up[..., :half], "row", shift_pairs(n_row, nz, 1, 2))
            last_down = lax.ppermute(lane_down[..., half:], "row", shift_pairs(n_row, nz, 1, -2))
            pieces[nz // 2] = jnp.concatenate([last_up, last_down], axis=-1)
    return jnp.stack(pieces), z


def reduce_cols(value, n_col):
    ny = n_col // (X_HI * CORES)
    c = lax.axis_index("col")
    core = c % CORES
    y = (c // CORES) % ny
    x_hi = c // (CORES * ny)
    send = jnp.take(value, 1 - core, axis=2)
    keep = jnp.take(value, core, axis=2)
    value = keep + lax.ppermute(send, "col", [(p, p ^ 1) for p in range(n_col)])
    rows = value.shape[2]
    upper = value[:, :, : rows // 2]
    lower = value[:, :, rows // 2 :]
    up = shift_pairs(n_col, ny, CORES, 1)
    down = shift_pairs(n_col, ny, CORES, -1)
    acc_up = jnp.take(upper, (y - 1) % ny, axis=1)
    acc_down = jnp.take(lower, (y + 1) % ny, axis=1)
    for s in range(1, ny):
        acc_up = lax.ppermute(acc_up, "col", up) + jnp.take(upper, (y - s - 1) % ny, axis=1)
        acc_down = lax.ppermute(acc_down, "col", down) + jnp.take(lower, (y + s + 1) % ny, axis=1)
    value = jnp.concatenate([acc_up, acc_down], axis=1)
    send = jnp.take(value, 1 - x_hi, axis=0)
    keep = jnp.take(value, x_hi, axis=0)
    half = n_col // X_HI
    return keep + lax.ppermute(send, "col", [(p, (p + half) % n_col) for p in range(n_col)])


def reduce_cols_a2a(value, n_col):
    chips = n_col // CORES
    rows = value.shape[0] // n_col
    core = lax.axis_index("col") % CORES
    value = value.reshape(chips, CORES, rows, *value.shape[1:])
    partner_pairs = [(p, p ^ 1) for p in range(n_col)]
    send = lax.dynamic_index_in_dim(value, 1 - core, axis=1, keepdims=False)
    keep = lax.dynamic_index_in_dim(value, core, axis=1, keepdims=False)
    summed = keep + lax.ppermute(send, "col", partner_pairs)
    groups = [list(range(e, n_col, CORES)) for e in range(CORES)]
    received = lax.all_to_all(summed, "col", 0, 0, tiled=True, axis_index_groups=groups)
    return jnp.sum(received, axis=0)


def local(anc_inv, factors_first, factors_second, lists_first, lists_second, parents, parent_link):
    n_row = lax.axis_size("row")
    n_col = lax.axis_size("col")
    local_rows, local_cols = anc_inv.shape
    n_first = factors_first.shape[0]
    n_second = factors_second.shape[0]
    members = n_first + n_second
    share_rows = factors_first.shape[1]
    panel_width = parent_link.shape[1]
    nz = n_row // X_LO
    row_anchor = lax.axis_index("row") * local_rows
    col_anchor = lax.axis_index("col") * local_cols
    out_first = tile_flags(lists_first, row_anchor, local_rows, panel_width)
    out_second = tile_flags(lists_second, row_anchor, local_rows, panel_width)
    panels = jnp.concatenate([factors_first, factors_second], axis=0)
    stacked = jnp.transpose(panels, (1, 0, 2)).reshape(share_rows, members * local_cols)
    pieces, z = gather_rows(stacked, n_row)
    col_mask = jnp.concatenate(
        [
            tile_flags(lists_first, col_anchor, local_cols, panel_width),
            tile_flags(lists_second, col_anchor, local_cols, panel_width),
        ],
        axis=0,
    )
    pieces = pieces.reshape(nz, X_LO, share_rows, members, local_cols) * col_mask
    partial_value = jnp.einsum(
        "tlkmj,ij->ltkmi", pieces, anc_inv, precision=high, preferred_element_type=jnp.float32
    )
    partial_value = jnp.roll(partial_value, z, axis=1)
    partial_value = partial_value.reshape(panel_width, members, local_rows)
    first_partial = partial_value[:, :n_first]
    chosen = jnp.take(first_partial, parents, axis=1)
    chosen_mask = jnp.take(out_first, parents, axis=0)
    coupling = jnp.einsum("cqk,qci->kci", parent_link, chosen, precision=high)
    second_partial = partial_value[:, n_first:] - chosen_mask[None, :, :] * coupling
    combined = jnp.concatenate([first_partial, second_partial], axis=1)
    reduced = reduce_cols_a2a(combined, n_col)
    reduced = jnp.transpose(reduced, (1, 0, 2))
    first_cols = -out_first[:, None, :] * reduced[:n_first]
    second_cols = -out_second[:, None, :] * reduced[n_first:]
    return (first_cols, second_cols)


def solution(mesh):
    in_specs = (P("row", "col"), P(None, "row", "col"), P(None, "row", "col"), P(), P(), P(), P())
    out_specs = (P(None, "col", "row"), P(None, "col", "row"))
    return jax.shard_map(local, mesh=mesh, in_specs=in_specs, out_specs=out_specs, check_vma=False)
```

```python
import jax
import jax.numpy as jnp
from jax import lax
from jax.sharding import PartitionSpec as P

high = lax.Precision.HIGH

X_LO = 2
X_HI = 2
CORES = 2


def tile_flags(block_lists, anchor, extent, tile_height):
    tile_ids = (anchor + jnp.arange(extent, dtype=jnp.int32)) // tile_height
    matches = block_lists[:, :, None] == tile_ids[None, None, :]
    return jnp.any(matches, axis=1).astype(jnp.float32)


def shift_pairs(size, inner, stride, shift):
    pairs = []
    for p in range(size):
        q = (p // stride) % inner
        target = p + (((q + shift) % inner) - q) * stride
        pairs.append((p, target))
    return pairs


def gather_rows(block, n_row):
    nz = n_row // X_LO
    r = lax.axis_index("row")
    x_lo = r // nz
    z = r % nz
    partner = lax.ppermute(block, "row", [(p, (p + nz) % n_row) for p in range(n_row)])
    pair = jnp.where(x_lo == 0, jnp.stack([block, partner]), jnp.stack([partner, block]))
    pieces = [None] * nz
    pieces[0] = pair
    steps = nz // 4
    half = pair.shape[-1] // 2
    lane_up = pair
    lane_down = pair
    for t in range(1, steps + 1):
        pieces[nz - (2 * t - 1)] = lax.ppermute(lane_up, "row", shift_pairs(n_row, nz, 1, 1))
        pieces[2 * t - 1] = lax.ppermute(lane_down, "row", shift_pairs(n_row, nz, 1, -1))
        if t < steps:
            lane_up = lax.ppermute(lane_up, "row", shift_pairs(n_row, nz, 1, 2))
            lane_down = lax.ppermute(lane_down, "row", shift_pairs(n_row, nz, 1, -2))
            pieces[nz - 2 * t] = lane_up
            pieces[2 * t] = lane_down
        else:
            last_up = lax.ppermute(lane_up[..., :half], "row", shift_pairs(n_row, nz, 1, 2))
            last_down = lax.ppermute(lane_down[..., half:], "row", shift_pairs(n_row, nz, 1, -2))
            pieces[nz // 2] = jnp.concatenate([last_up, last_down], axis=-1)
    return jnp.stack(pieces), z


def reduce_cols(value, n_col):
    ny = n_col // (X_HI * CORES)
    c = lax.axis_index("col")
    core = c % CORES
    y = (c // CORES) % ny
    x_hi = c // (CORES * ny)
    send = jnp.take(value, 1 - core, axis=2)
    keep = jnp.take(value, core, axis=2)
    value = keep + lax.ppermute(send, "col", [(p, p ^ 1) for p in range(n_col)])
    rows = value.shape[2]
    upper = value[:, :, : rows // 2]
    lower = value[:, :, rows // 2 :]
    up = shift_pairs(n_col, ny, CORES, 1)
    down = shift_pairs(n_col, ny, CORES, -1)
    acc_up = jnp.take(upper, (y - 1) % ny, axis=1)
    acc_down = jnp.take(lower, (y + 1) % ny, axis=1)
    for s in range(1, ny):
        acc_up = lax.ppermute(acc_up, "col", up) + jnp.take(upper, (y - s - 1) % ny, axis=1)
        acc_down = lax.ppermute(acc_down, "col", down) + jnp.take(lower, (y + s + 1) % ny, axis=1)
    value = jnp.concatenate([acc_up, acc_down], axis=1)
    send = jnp.take(value, 1 - x_hi, axis=0)
    keep = jnp.take(value, x_hi, axis=0)
    half = n_col // X_HI
    return keep + lax.ppermute(send, "col", [(p, (p + half) % n_col) for p in range(n_col)])


def reduce_cols_a2a(value, n_col):
    chips = n_col // CORES
    rows = value.shape[0] // n_col
    core = lax.axis_index("col") % CORES
    value = value.reshape(chips, CORES, rows, *value.shape[1:])
    partner_pairs = [(p, p ^ 1) for p in range(n_col)]
    send = lax.dynamic_index_in_dim(value, 1 - core, axis=1, keepdims=False)
    keep = lax.dynamic_index_in_dim(value, core, axis=1, keepdims=False)
    summed = keep + lax.ppermute(send, "col", partner_pairs)
    groups = [list(range(e, n_col, CORES)) for e in range(CORES)]
    received = lax.all_to_all(summed, "col", 0, 0, tiled=True, axis_index_groups=groups)
    return jnp.sum(received, axis=0)


def local(anc_inv, factors_first, factors_second, lists_first, lists_second, parents, parent_link):
    n_row = lax.axis_size("row")
    n_col = lax.axis_size("col")
    local_rows, local_cols = anc_inv.shape
    n_first = factors_first.shape[0]
    n_second = factors_second.shape[0]
    members = n_first + n_second
    share_rows = factors_first.shape[1]
    panel_width = parent_link.shape[1]
    nz = n_row // X_LO
    row_anchor = lax.axis_index("row") * local_rows
    col_anchor = lax.axis_index("col") * local_cols
    out_first = tile_flags(lists_first, row_anchor, local_rows, panel_width)
    out_second = tile_flags(lists_second, row_anchor, local_rows, panel_width)
    panels = jnp.concatenate([factors_first, factors_second], axis=0)
    stacked = jnp.transpose(panels, (1, 0, 2)).reshape(share_rows, members * local_cols)
    pieces, z = gather_rows(stacked, n_row)
    col_mask = jnp.concatenate(
        [
            tile_flags(lists_first, col_anchor, local_cols, panel_width),
            tile_flags(lists_second, col_anchor, local_cols, panel_width),
        ],
        axis=0,
    )
    pieces = pieces.reshape(nz, X_LO, share_rows, members, local_cols) * col_mask
    partial_value = jnp.einsum(
        "tlkmj,ij->ltkmi", pieces, anc_inv, precision=high, preferred_element_type=jnp.float32
    )
    partial_value = jnp.roll(partial_value, z, axis=1)
    partial_value = partial_value.reshape(panel_width, members, local_rows)
    first_partial = partial_value[:, :n_first]
    chosen = jnp.stack(
        [lax.dynamic_index_in_dim(first_partial, parents[c], axis=1, keepdims=False) for c in range(n_second)],
        axis=1,
    )
    chosen_mask = jnp.take(out_first, parents, axis=0)
    coupling = jnp.einsum("cqk,qci->kci", parent_link, chosen, precision=high)
    second_partial = partial_value[:, n_first:] - chosen_mask[None, :, :] * coupling
    combined = jnp.concatenate([first_partial, second_partial], axis=1)
    reduced = reduce_cols_a2a(combined, n_col)
    reduced = jnp.transpose(reduced, (1, 0, 2))
    first_cols = -out_first[:, None, :] * reduced[:n_first]
    second_cols = -out_second[:, None, :] * reduced[n_first:]
    return (first_cols, second_cols)


def solution(mesh):
    in_specs = (P("row", "col"), P(None, "row", "col"), P(None, "row", "col"), P(), P(), P(), P())
    out_specs = (P(None, "col", "row"), P(None, "col", "row"))
    return jax.shard_map(local, mesh=mesh, in_specs=in_specs, out_specs=out_specs, check_vma=False)
```
